32 devices in a mesh: groups: 2 (over y), seq: 4 (over z), chan: 4 (over x, core).
Axes of the slice: x: 2, y: 2, z: 4, core: 2. Of those that a mesh axis runs over, the one named last changes fastest.
Arguments:
- outer_gate: bfloat16 [1024, 8192], P(('groups', 'seq'), 'chan'), parts along dimension 0, may hold values from -6 to 6
- inner_gate: bfloat16 [1024, 8192], P(('groups', 'seq'), 'chan'), parts along dimension 0, may hold values from -6 to 6
- signal: bfloat16 [1024, 8192], P(('groups', 'seq'), 'chan'), parts along dimension 0, may hold values from -6 to 6
- filter_in: float32 [33, 64], replicated, may hold values from -1 to 1
- filter_bias: float32 [64], replicated, may hold values from -3.140625 to 3.140625
- filter_out: float32 [64, 512], P(None, 'chan'), may hold values from -0.75 to 0.75
- decay: float32 [512], P('chan'), may hold values from 0.000390625 to 0.05
- skip_gain: float32 [8192], P('chan'), may hold values from -4 to 4
Outputs:
- mixed: bfloat16 [1024, 8192], P(('groups', 'seq'), 'chan'), parts along dimension 0
The draws below stay inside these ranges and needn't reach their ends.
There are 2 independent parts, one for each index of `groups`. The reference program is written for one: setup_inputs(seed, part) draws one part's arguments, and reference() takes and returns one part's arrays. A program takes and returns all parts, laid end to end along the dimension named above; an argument that names none is the same for every part. Nothing has to cross between parts.
All inputs are finite; a program needn't handle non-finite values.
Results may differ from the reference program's by a relative error of at most 0.0052.
Values may be sent and summed in bfloat16 or wider, within the bound.
No kernel may reach another device: no remote copies, remote signals or barrier semaphores. Data moves between devices by JAX's collectives and lax.ppermute only.
A program may use at most 64 MiB of HBM per device.

```python
import math
import jax
import jax.numpy as jnp
from jax import lax

D = 8192
GROUP = 16
FILTERS = 512
FW = 64
BANDS = 16
EMB = 33
TOKENS = 512


def draw_decay(key, part):
    pick_key, slow_key, fast_key = jax.random.split(key, 3)
    share = 0.5
    keep = jax.random.uniform(pick_key, (FILTERS,), jnp.float32) < share
    slow = jnp.exp(jax.random.uniform(slow_key, (FILTERS,), jnp.float32, math.log(0.2 / TOKENS), math.log(2.3 / TOKENS)))
    fast = jnp.exp(jax.random.uniform(fast_key, (FILTERS,), jnp.float32, math.log(2.3 / TOKENS), math.log(0.05)))
    return jnp.where(keep, slow, fast).astype(jnp.float32)


def shard_levels(key, dims, cuts, least, largest):
    loudness, own = 1.0, jax.random.fold_in(key, 6)
    for axis_at, parts in cuts:
        heights = jnp.exp(jax.random.uniform(jax.random.fold_in(own, axis_at), (parts,), jnp.float32, least / len(cuts), largest / len(cuts)))
        loudness = loudness * jnp.repeat(heights, dims[axis_at] // parts).reshape([-1 if axis == axis_at else 1 for axis in range(len(dims))])
    return loudness


def centred(rng, shape, width, reach, pieces=(), held_as=jnp.bfloat16):
    factor_of = shard_levels(rng, shape, pieces, -0.22, 0.18) if pieces else 1.0
    values = jax.random.normal(rng, shape, jnp.float32) * width * factor_of
    return jnp.minimum(jnp.maximum(values, -reach), reach).astype(held_as)


def setup_inputs(seed: int = 0, part: int = 0) -> dict:
    key_list = jax.random.split(jax.random.key(seed), 9)
    own_keys = jax.random.split(jax.random.fold_in(key_list[8], part), 9)
    return {
        "outer_gate": centred(own_keys[0], (TOKENS, D), 1.0, 6.0, ((0, 4), (1, 4))),
        "inner_gate": centred(own_keys[1], (TOKENS, D), 1.0, 6.0, ((0, 4), (1, 4))),
        "signal": centred(own_keys[2], (TOKENS, D), 1.0, 6.0, ((0, 4), (1, 4))),
        "filter_in": centred(key_list[3], (EMB, FW), EMB ** -0.5, 1.0, (), jnp.float32),
        "filter_bias": jnp.clip(jax.random.uniform(key_list[4], (FW,), jnp.float32, -3.140625, 3.140625), -3.140625, 3.140625),
        "filter_out": centred(key_list[5], (FW, FILTERS), FW ** -0.5, 0.75, ((1, 4),), jnp.float32),
        "decay": draw_decay(jax.random.fold_in(key_list[8], 71), part),
        "skip_gain": centred(key_list[7], (D,), 1.0, 4.0, ((0, 4),), jnp.float32),
    }


def filter_table(positions, total, filter_in, filter_bias, filter_out, decay):
    bands = 2.8 * 0.7 ** jnp.arange(BANDS, dtype=jnp.float32)
    angles = positions[:, None] * bands[None, :]
    feats = jnp.concatenate([(positions / total)[:, None], jnp.cos(angles), jnp.sin(angles)], axis=1)
    hidden = jnp.sin(10.0 * (jnp.dot(feats, filter_in, precision=lax.Precision.HIGHEST) + filter_bias[None, :]))
    raw = jnp.dot(hidden, filter_out, precision=lax.Precision.HIGHEST)
    envelope = jnp.sqrt(2.0 * decay)[None, :] * jnp.exp(-decay[None, :] * positions[:, None])
    return (raw * envelope).astype(jnp.bfloat16)

def reference(outer_gate, inner_gate, signal, filter_in, filter_bias, filter_out, decay, skip_gain):
    positions = jnp.arange(TOKENS, dtype=jnp.int32).astype(jnp.float32)
    filters = filter_table(positions, float(TOKENS), filter_in, filter_bias, filter_out, decay)
    gated = (inner_gate.astype(jnp.float32) * signal.astype(jnp.float32)).astype(jnp.bfloat16)
    span = 2 * TOKENS
    wide = gated.astype(jnp.float32).reshape(TOKENS, FILTERS, GROUP)
    spectrum = jnp.fft.rfft(wide, n=span, axis=0)
    response = jnp.fft.rfft(filters.astype(jnp.float32), n=span, axis=0)
    conv = jnp.fft.irfft(spectrum * response[:, :, None], n=span, axis=0)[:TOKENS]
    conv = conv.reshape(TOKENS, D)
    mixed = outer_gate.astype(jnp.float32) * (conv + skip_gain[None, :] * gated.astype(jnp.float32))
    return mixed.astype(jnp.bfloat16)
```

```python
import functools

import jax
import jax.numpy as jnp
from jax import lax
from jax.experimental import pallas as pl
from jax.experimental.pallas import tpu as pltpu
from jax.sharding import PartitionSpec as P

GROUP = 16
BANDS = 16
FILTERS_PER_STEP = 8


def filter_table(positions, total, filter_in, filter_bias, filter_out, decay):
    bands = 2.8 * 0.7 ** jnp.arange(BANDS, dtype=jnp.float32)
    angles = positions[:, None] * bands[None, :]
    feats = jnp.concatenate(
        [(positions / total)[:, None], jnp.cos(angles), jnp.sin(angles)], axis=1
    )
    hidden = jnp.sin(
        10.0 * (jnp.dot(feats, filter_in, precision=lax.Precision.HIGHEST) + filter_bias[None, :])
    )
    raw = jnp.dot(hidden, filter_out, precision=lax.Precision.HIGHEST)
    envelope = jnp.sqrt(2.0 * decay)[None, :] * jnp.exp(-decay[None, :] * positions[:, None])
    return (raw * envelope).astype(jnp.bfloat16)


def toeplitz_kernel(s_ref, filt_ref, x_ref, o_ref, *, block, own):
    fb = filt_ref.shape[1]
    s = s_ref[0]
    upper = (lax.broadcasted_iota(jnp.int32, (block, block), 1)
             >= lax.broadcasted_iota(jnp.int32, (block, block), 0))

    def rolled(g, k):
        w = filt_ref[k + 1, pl.ds(g, block, stride=0), :]
        return pltpu.roll(w, 0, 1, stride=1, stride_axis=0)

    for g in range(fb):
        rows = slice(g * GROUP, (g + 1) * GROUP)
        r0 = rolled(g, 0)
        if own:
            t0 = jnp.where(upper, r0, 0.0).astype(jnp.bfloat16)
            o_ref[rows, :] = jnp.dot(x_ref[0, rows, :], t0, preferred_element_type=jnp.float32)
        else:
            def body(d, carry):
                acc, prev = carry
                cur = rolled(g, d)
                t = jnp.where(upper, cur, prev).astype(jnp.bfloat16)
                acc = acc + jnp.dot(x_ref[s - d, rows, :], t, preferred_element_type=jnp.float32)
                return acc, cur

            acc0 = jnp.zeros((GROUP, block), jnp.float32)
            acc, _ = lax.fori_loop(1, s + 1, body, (acc0, r0))
            o_ref[rows, :] = acc


def toeplitz_conv(s, filt, x, own):
    nb, chans, block = x.shape
    count = filt.shape[1]
    fb = FILTERS_PER_STEP
    kernel = functools.partial(toeplitz_kernel, block=block, own=own)
    return pl.pallas_call(
        kernel,
        out_shape=jax.ShapeDtypeStruct((chans, block), jnp.float32),
        grid_spec=pltpu.PrefetchScalarGridSpec(
            num_scalar_prefetch=1,
            grid=(count // fb,),
            in_specs=[
                pl.BlockSpec((filt.shape[0], fb, block), lambda i, s_: (0, i, 0)),
                pl.BlockSpec((nb, fb * GROUP, block), lambda i, s_: (0, i, 0)),
            ],
            out_specs=pl.BlockSpec((fb * GROUP, block), lambda i, s_: (i, 0)),
        ),
    )(s, filt, x)


def per_device(
    outer_gate, inner_gate, signal, filter_in, filter_bias, filter_out, decay, skip_gain
):
    own_rows = signal.shape[0]
    nb = lax.axis_size("seq")
    total_rows = own_rows * nb
    s = lax.axis_index("seq")
    gated = (inner_gate.astype(jnp.float32) * signal.astype(jnp.float32)).astype(jnp.bfloat16)
    gated_t = gated.T
    positions = jnp.arange(total_rows, dtype=jnp.int32).astype(jnp.float32)
    filters = filter_table(positions, float(total_rows), filter_in, filter_bias, filter_out, decay)
    count = filters.shape[1]
    lagged = filters.astype(jnp.float32).reshape(nb, own_rows, count).transpose(0, 2, 1)
    filt = jnp.concatenate([jnp.zeros((1, count, own_rows), jnp.float32), lagged], axis=0)
    s_arr = jnp.reshape(s, (1,)).astype(jnp.int32)
    own = toeplitz_conv(s_arr, filt, gated_t[None], True)
    gathered = lax.all_gather(gated_t, "seq", axis=0, tiled=False)
    rest = toeplitz_conv(s_arr, filt, gathered, False)
    conv = (own + rest).T
    mixed = outer_gate.astype(jnp.float32) * (conv + skip_gain[None, :] * gated.astype(jnp.float32))
    return mixed.astype(jnp.bfloat16)


def solution(mesh):
    placed = (
        P(("groups", "seq"), "chan"),
        P(("groups", "seq"), "chan"),
        P(("groups", "seq"), "chan"),
        P(),
        P(),
        P(None, "chan"),
        P("chan"),
        P("chan"),
    )
    return jax.shard_map(
        per_device,
        mesh=mesh,
        in_specs=placed,
        out_specs=P(("groups", "seq"), "chan"),
        check_vma=False,
    )
```

```python
import functools

import jax
import jax.numpy as jnp
from jax import lax
from jax.experimental import pallas as pl
from jax.experimental.pallas import tpu as pltpu
from jax.sharding import PartitionSpec as P

GROUP = 16
BANDS = 16
FILTERS_PER_STEP = 8


def filter_table(positions, total, filter_in, filter_bias, filter_out, decay):
    bands = 2.8 * 0.7 ** jnp.arange(BANDS, dtype=jnp.float32)
    angles = positions[:, None] * bands[None, :]
    feats = jnp.concatenate(
        [(positions / total)[:, None], jnp.cos(angles), jnp.sin(angles)], axis=1
    )
    hidden = jnp.sin(
        10.0 * (jnp.dot(feats, filter_in, precision=lax.Precision.HIGHEST) + filter_bias[None, :])
    )
    raw = jnp.dot(hidden, filter_out, precision=lax.Precision.HIGHEST)
    envelope = jnp.sqrt(2.0 * decay)[None, :] * jnp.exp(-decay[None, :] * positions[:, None])
    return (raw * envelope).astype(jnp.bfloat16)


def toeplitz_kernel(filt_ref, x_ref, o_ref, acc_ref):
    nb = x_ref.shape[1] // GROUP
    fb = x_ref.shape[0]
    block = x_ref.shape[2]
    upper = (lax.broadcasted_iota(jnp.int32, (block, block), 1)
             >= lax.broadcasted_iota(jnp.int32, (block, block), 0))
    for g in range(fb):
        acc_ref[...] = jnp.zeros(acc_ref.shape, jnp.float32)
        prev = None
        for d in range(nb):
            w = filt_ref[d + 1, pl.ds(g, block, stride=0), :]
            cur = pltpu.roll(w, 0, 1, stride=1, stride_axis=0)
            low = 0.0 if prev is None else prev
            t = jnp.where(upper, cur, low).astype(jnp.bfloat16)
            rows = (nb - d) * GROUP
            acc_ref[d * GROUP:, :] += jnp.dot(
                x_ref[g, :rows, :], t, preferred_element_type=jnp.float32
            )
            prev = cur
        for i in range(nb):
            o_ref[i, g * GROUP:(g + 1) * GROUP, :] = acc_ref[i * GROUP:(i + 1) * GROUP, :]


def toeplitz_conv(filt, x):
    count, rows, block = x.shape
    nb = rows // GROUP
    fb = min(FILTERS_PER_STEP, count)
    return pl.pallas_call(
        toeplitz_kernel,
        out_shape=jax.ShapeDtypeStruct((nb, count * GROUP, block), jnp.float32),
        grid=(count // fb,),
        in_specs=[
            pl.BlockSpec((nb + 1, fb, block), lambda i: (0, i, 0)),
            pl.BlockSpec((fb, rows, block), lambda i: (i, 0, 0)),
        ],
        out_specs=pl.BlockSpec((nb, fb * GROUP, block), lambda i: (0, i, 0)),
        scratch_shapes=[pltpu.VMEM((rows, block), jnp.float32)],
    )(filt, x)


def per_device(
    outer_gate, inner_gate, signal, filter_in, filter_bias, filter_out, decay, skip_gain
):
    own_rows, width = signal.shape
    nb = lax.axis_size("seq")
    total_rows = own_rows * nb
    s = lax.axis_index("seq")
    count = width // GROUP
    sub = count // nb
    gated = (inner_gate.astype(jnp.float32) * signal.astype(jnp.float32)).astype(jnp.bfloat16)
    gated_t = gated.T.reshape(nb, sub, GROUP, own_rows)
    got = lax.all_to_all(gated_t, "seq", 0, 0, tiled=False)
    x = got.transpose(1, 0, 2, 3).reshape(sub, nb * GROUP, own_rows)
    positions = jnp.arange(total_rows, dtype=jnp.int32).astype(jnp.float32)
    my_out = lax.dynamic_slice_in_dim(filter_out, s * sub, sub, 1)
    my_decay = lax.dynamic_slice_in_dim(decay, s * sub, sub, 0)
    filters = filter_table(positions, float(total_rows), filter_in, filter_bias, my_out, my_decay)
    lagged = filters.astype(jnp.float32).reshape(nb, own_rows, sub).transpose(0, 2, 1)
    filt = jnp.concatenate([jnp.zeros((1, sub, own_rows), jnp.float32), lagged], axis=0)
    conv_parts = toeplitz_conv(filt, x)
    back = lax.all_to_all(conv_parts, "seq", 0, 0, tiled=False)
    conv = back.reshape(width, own_rows).T
    mixed = outer_gate.astype(jnp.float32) * (conv + skip_gain[None, :] * gated.astype(jnp.float32))
    return mixed.astype(jnp.bfloat16)


def solution(mesh):
    placed = (
        P(("groups", "seq"), "chan"),
        P(("groups", "seq"), "chan"),
        P(("groups", "seq"), "chan"),
        P(),
        P(),
        P(None, "chan"),
        P("chan"),
        P("chan"),
    )
    return jax.shard_map(
        per_device,
        mesh=mesh,
        in_specs=placed,
        out_specs=P(("groups", "seq"), "chan"),
        check_vma=False,
    )
```

```python
import functools

import jax
import jax.numpy as jnp
from jax import lax
from jax.experimental import pallas as pl
from jax.experimental.pallas import tpu as pltpu
from jax.sharding import PartitionSpec as P

GROUP = 16
BANDS = 16
FILTERS_PER_STEP = 8


def filter_table(positions, total, filter_in, filter_bias, filter_out, decay):
    bands = 2.8 * 0.7 ** jnp.arange(BANDS, dtype=jnp.float32)
    angles = positions[:, None] * bands[None, :]
    feats = jnp.concatenate(
        [(positions / total)[:, None], jnp.cos(angles), jnp.sin(angles)], axis=1
    )
    hidden = jnp.sin(
        10.0 * (jnp.dot(feats, filter_in, precision=lax.Precision.HIGHEST) + filter_bias[None, :])
    )
    raw = jnp.dot(hidden, filter_out, precision=lax.Precision.HIGHEST)
    envelope = jnp.sqrt(2.0 * decay)[None, :] * jnp.exp(-decay[None, :] * positions[:, None])
    return (raw * envelope).astype(jnp.bfloat16)


def toeplitz_kernel(filt_ref, x_ref, outer_ref, skip_ref, o_ref, acc_ref):
    nb = x_ref.shape[1] // GROUP
    fb = x_ref.shape[0]
    block = x_ref.shape[2]
    upper = (lax.broadcasted_iota(jnp.int32, (block, block), 1)
             >= lax.broadcasted_iota(jnp.int32, (block, block), 0))
    for g in range(fb):
        acc_ref[...] = jnp.zeros(acc_ref.shape, jnp.float32)
        prev = None
        for d in range(nb):
            w = filt_ref[d + 1, pl.ds(g, block, stride=0), :]
            cur = pltpu.roll(w, 0, 1, stride=1, stride_axis=0)
            low = 0.0 if prev is None else prev
            t = jnp.where(upper, cur, low).astype(jnp.bfloat16)
            rows = (nb - d) * GROUP
            acc_ref[d * GROUP:, :] += jnp.dot(
                x_ref[g, :rows, :], t, preferred_element_type=jnp.float32
            )
            prev = cur
        ch = slice(g * GROUP, (g + 1) * GROUP)
        skip = skip_ref[ch, :]
        for i in range(nb):
            blk = slice(i * GROUP, (i + 1) * GROUP)
            inner = acc_ref[blk, :] + skip * x_ref[g, blk, :].astype(jnp.float32)
            o_ref[i, ch, :] = (outer_ref[i, ch, :].astype(jnp.float32) * inner).astype(jnp.bfloat16)


def toeplitz_conv(filt, x, outer, skip):
    count, rows, block = x.shape
    nb = rows // GROUP
    fb = min(FILTERS_PER_STEP, count)
    return pl.pallas_call(
        toeplitz_kernel,
        out_shape=jax.ShapeDtypeStruct((nb, count * GROUP, block), jnp.bfloat16),
        grid=(count // fb,),
        in_specs=[
            pl.BlockSpec((nb + 1, fb, block), lambda i: (0, i, 0)),
            pl.BlockSpec((fb, rows, block), lambda i: (i, 0, 0)),
            pl.BlockSpec((nb, fb * GROUP, block), lambda i: (0, i, 0)),
            pl.BlockSpec((fb * GROUP, 1), lambda i: (i, 0)),
        ],
        out_specs=pl.BlockSpec((nb, fb * GROUP, block), lambda i: (0, i, 0)),
        scratch_shapes=[pltpu.VMEM((rows, block), jnp.float32)],
    )(filt, x, outer, skip)


def per_device(
    outer_gate, inner_gate, signal, filter_in, filter_bias, filter_out, decay, skip_gain
):
    own_rows, width = signal.shape
    nb = lax.axis_size("seq")
    total_rows = own_rows * nb
    s = lax.axis_index("seq")
    count = width // GROUP
    sub = count // nb
    gated = (inner_gate.astype(jnp.float32) * signal.astype(jnp.float32)).astype(jnp.bfloat16)
    both = jnp.stack([outer_gate.T, gated.T]).reshape(2, nb, sub * GROUP, own_rows)
    got = lax.all_to_all(both.transpose(1, 0, 2, 3), "seq", 0, 0, tiled=False)
    outer_got = got[:, 0]
    x = got[:, 1].reshape(nb, sub, GROUP, own_rows).transpose(1, 0, 2, 3).reshape(
        sub, nb * GROUP, own_rows)
    positions = jnp.arange(total_rows, dtype=jnp.int32).astype(jnp.float32)
    my_out = lax.dynamic_slice_in_dim(filter_out, s * sub, sub, 1)
    my_decay = lax.dynamic_slice_in_dim(decay, s * sub, sub, 0)
    filters = filter_table(positions, float(total_rows), filter_in, filter_bias, my_out, my_decay)
    lagged = filters.astype(jnp.float32).reshape(nb, own_rows, sub).transpose(0, 2, 1)
    filt = jnp.concatenate([jnp.zeros((1, sub, own_rows), jnp.float32), lagged], axis=0)
    my_skip = lax.dynamic_slice_in_dim(skip_gain, s * sub * GROUP, sub * GROUP, 0)[:, None]
    mixed_parts = toeplitz_conv(filt, x, outer_got, my_skip)
    back = lax.all_to_all(mixed_parts, "seq", 0, 0, tiled=False)
    return back.reshape(width, own_rows).T


def solution(mesh):
    placed = (
        P(("groups", "seq"), "chan"),
        P(("groups", "seq"), "chan"),
        P(("groups", "seq"), "chan"),
        P(),
        P(),
        P(None, "chan"),
        P("chan"),
        P("chan"),
    )
    return jax.shard_map(
        per_device,
        mesh=mesh,
        in_specs=placed,
        out_specs=P(("groups", "seq"), "chan"),
        check_vma=False,
    )
```

```python
import functools

import jax
import jax.numpy as jnp
from jax import lax
from jax.experimental import pallas as pl
from jax.experimental.pallas import tpu as pltpu
from jax.sharding import PartitionSpec as P

GROUP = 16
BANDS = 16
FILTERS_PER_STEP = 8


def filter_table(positions, total, filter_in, filter_bias, filter_out, decay):
    bands = 2.8 * 0.7 ** jnp.arange(BANDS, dtype=jnp.float32)
    angles = positions[:, None] * bands[None, :]
    feats = jnp.concatenate(
        [(positions / total)[:, None], jnp.cos(angles), jnp.sin(angles)], axis=1
    )
    hidden = jnp.sin(
        10.0 * (jnp.dot(feats, filter_in, precision=lax.Precision.HIGHEST) + filter_bias[None, :])
    )
    raw = jnp.dot(hidden, filter_out, precision=lax.Precision.HIGHEST)
    envelope = jnp.sqrt(2.0 * decay)[None, :] * jnp.exp(-decay[None, :] * positions[:, None])
    return (raw * envelope).astype(jnp.bfloat16)


def toeplitz_kernel(filt_ref, x_ref, o_ref, acc_ref):
    nb = x_ref.shape[1] // GROUP
    fb = x_ref.shape[0]
    block = x_ref.shape[2]
    upper = (lax.broadcasted_iota(jnp.int32, (block, block), 1)
             >= lax.broadcasted_iota(jnp.int32, (block, block), 0))
    for g in range(fb):
        acc_ref[...] = jnp.zeros(acc_ref.shape, jnp.float32)
        prev = None
        for d in range(nb):
            w = filt_ref[d + 1, pl.ds(g, block, stride=0), :]
            cur = pltpu.roll(w, 0, 1, stride=1, stride_axis=0)
            low = 0.0 if prev is None else prev
            t = jnp.where(upper, cur, low).astype(jnp.bfloat16)
            rows = (nb - d) * GROUP
            acc_ref[d * GROUP:, :] += jnp.dot(
                x_ref[g, :rows, :], t, preferred_element_type=jnp.float32
            )
            prev = cur
        for i in range(nb):
            o_ref[i, g * GROUP:(g + 1) * GROUP, :] = (
                acc_ref[i * GROUP:(i + 1) * GROUP, :].astype(jnp.bfloat16))


def toeplitz_conv(filt, x):
    count, rows, block = x.shape
    nb = rows // GROUP
    fb = min(FILTERS_PER_STEP, count)
    return pl.pallas_call(
        toeplitz_kernel,
        out_shape=jax.ShapeDtypeStruct((nb, count * GROUP, block), jnp.bfloat16),
        grid=(count // fb,),
        in_specs=[
            pl.BlockSpec((nb + 1, fb, block), lambda i: (0, i, 0)),
            pl.BlockSpec((fb, rows, block), lambda i: (i, 0, 0)),
        ],
        out_specs=pl.BlockSpec((nb, fb * GROUP, block), lambda i: (0, i, 0)),
        scratch_shapes=[pltpu.VMEM((rows, block), jnp.float32)],
    )(filt, x)


def per_device(
    outer_gate, inner_gate, signal, filter_in, filter_bias, filter_out, decay, skip_gain
):
    own_rows, width = signal.shape
    nb = lax.axis_size("seq")
    total_rows = own_rows * nb
    s = lax.axis_index("seq")
    count = width // GROUP
    sub = count // nb
    gated = (inner_gate.astype(jnp.float32) * signal.astype(jnp.float32)).astype(jnp.bfloat16)
    gated_t = gated.T.reshape(nb, sub, GROUP, own_rows)
    got = lax.all_to_all(gated_t, "seq", 0, 0, tiled=False)
    x = got.transpose(1, 0, 2, 3).reshape(sub, nb * GROUP, own_rows)
    positions = jnp.arange(total_rows, dtype=jnp.int32).astype(jnp.float32)
    my_out = lax.dynamic_slice_in_dim(filter_out, s * sub, sub, 1)
    my_decay = lax.dynamic_slice_in_dim(decay, s * sub, sub, 0)
    filters = filter_table(positions, float(total_rows), filter_in, filter_bias, my_out, my_decay)
    lagged = filters.astype(jnp.float32).reshape(nb, own_rows, sub).transpose(0, 2, 1)
    filt = jnp.concatenate([jnp.zeros((1, sub, own_rows), jnp.float32), lagged], axis=0)
    conv_parts = toeplitz_conv(filt, x)
    back = lax.all_to_all(conv_parts, "seq", 0, 0, tiled=False)
    conv = back.reshape(width, own_rows).T.astype(jnp.float32)
    mixed = outer_gate.astype(jnp.float32) * (conv + skip_gain[None, :] * gated.astype(jnp.float32))
    return mixed.astype(jnp.bfloat16)


def solution(mesh):
    placed = (
        P(("groups", "seq"), "chan"),
        P(("groups", "seq"), "chan"),
        P(("groups", "seq"), "chan"),
        P(),
        P(),
        P(None, "chan"),
        P("chan"),
        P("chan"),
    )
    return jax.shard_map(
        per_device,
        mesh=mesh,
        in_specs=placed,
        out_specs=P(("groups", "seq"), "chan"),
        check_vma=False,
    )
```

```python
import functools

import jax
import jax.numpy as jnp
from jax import lax
from jax.experimental import pallas as pl
from jax.experimental.pallas import tpu as pltpu
from jax.sharding import PartitionSpec as P

GROUP = 16
BANDS = 16
FILTERS_PER_STEP = 8


def filter_table(positions, total, filter_in, filter_bias, filter_out, decay):
    bands = 2.8 * 0.7 ** jnp.arange(BANDS, dtype=jnp.float32)
    angles = positions[:, None] * bands[None, :]
    feats = jnp.concatenate(
        [(positions / total)[:, None], jnp.cos(angles), jnp.sin(angles)], axis=1
    )
    hidden = jnp.sin(
        10.0 * (jnp.dot(feats, filter_in, precision=lax.Precision.HIGHEST) + filter_bias[None, :])
    )
    raw = jnp.dot(hidden, filter_out, precision=lax.Precision.HIGHEST)
    envelope = jnp.sqrt(2.0 * decay)[None, :] * jnp.exp(-decay[None, :] * positions[:, None])
    return (raw * envelope).astype(jnp.bfloat16)


def toeplitz_kernel(filt_ref, x_ref, o_ref, acc_ref):
    nb = x_ref.shape[1] // GROUP
    fb = x_ref.shape[0]
    block = x_ref.shape[2]
    upper = (lax.broadcasted_iota(jnp.int32, (block, block), 1)
             >= lax.broadcasted_iota(jnp.int32, (block, block), 0))
    for g in range(fb):
        acc_ref[...] = jnp.zeros(acc_ref.shape, jnp.float32)
        prev = None
        for d in range(nb):
            w = filt_ref[d + 1, pl.ds(g, block, stride=0), :]
            cur = pltpu.roll(w, 0, 1, stride=1, stride_axis=0)
            low = 0.0 if prev is None else prev
            t = jnp.where(upper, cur, low).astype(jnp.bfloat16)
            rows = (nb - d) * GROUP
            acc_ref[d * GROUP:, :] += jnp.dot(
                x_ref[g, :rows, :], t, preferred_element_type=jnp.float32
            )
            prev = cur
        for i in range(nb):
            o_ref[i, g * GROUP:(g + 1) * GROUP, :] = (
                acc_ref[i * GROUP:(i + 1) * GROUP, :].astype(jnp.bfloat16))


def toeplitz_conv(filt, x):
    count, rows, block = x.shape
    nb = rows // GROUP
    fb = min(FILTERS_PER_STEP, count)
    return pl.pallas_call(
        toeplitz_kernel,
        out_shape=jax.ShapeDtypeStruct((nb, count * GROUP, block), jnp.bfloat16),
        grid=(count // fb,),
        in_specs=[
            pl.BlockSpec((nb + 1, fb, block), lambda i: (0, i, 0)),
            pl.BlockSpec((fb, rows, block), lambda i: (i, 0, 0)),
        ],
        out_specs=pl.BlockSpec((nb, fb * GROUP, block), lambda i: (0, i, 0)),
        scratch_shapes=[pltpu.VMEM((rows, block), jnp.float32)],
    )(filt, x)


def exchange(x, nb, s):
    got = [x[s]]
    for k in range(1, nb):
        piece = lax.dynamic_index_in_dim(x, (s + k) % nb, 0, keepdims=False)
        got.append(lax.ppermute(piece, "seq", [(i, (i + k) % nb) for i in range(nb)]))
    z = jnp.stack(got)
    order = (s - jnp.arange(nb, dtype=jnp.int32)) % nb
    return jnp.take(z, order, axis=0)


def per_device(
    outer_gate, inner_gate, signal, filter_in, filter_bias, filter_out, decay, skip_gain
):
    own_rows, width = signal.shape
    nb = lax.axis_size("seq")
    total_rows = own_rows * nb
    s = lax.axis_index("seq")
    count = width // GROUP
    sub = count // nb
    gated = (inner_gate.astype(jnp.float32) * signal.astype(jnp.float32)).astype(jnp.bfloat16)
    gated_t = gated.T.reshape(nb, sub, GROUP, own_rows)
    got = exchange(gated_t, nb, s)
    x = got.transpose(1, 0, 2, 3).reshape(sub, nb * GROUP, own_rows)
    positions = jnp.arange(total_rows, dtype=jnp.int32).astype(jnp.float32)
    my_out = lax.dynamic_slice_in_dim(filter_out, s * sub, sub, 1)
    my_decay = lax.dynamic_slice_in_dim(decay, s * sub, sub, 0)
    filters = filter_table(positions, float(total_rows), filter_in, filter_bias, my_out, my_decay)
    lagged = filters.astype(jnp.float32).reshape(nb, own_rows, sub).transpose(0, 2, 1)
    filt = jnp.concatenate([jnp.zeros((1, sub, own_rows), jnp.float32), lagged], axis=0)
    conv_parts = toeplitz_conv(filt, x)
    back = exchange(conv_parts, nb, s)
    conv = back.reshape(width, own_rows).T.astype(jnp.float32)
    mixed = outer_gate.astype(jnp.float32) * (conv + skip_gain[None, :] * gated.astype(jnp.float32))
    return mixed.astype(jnp.bfloat16)


def solution(mesh):
    placed = (
        P(("groups", "seq"), "chan"),
        P(("groups", "seq"), "chan"),
        P(("groups", "seq"), "chan"),
        P(),
        P(),
        P(None, "chan"),
        P("chan"),
        P("chan"),
    )
    return jax.shard_map(
        per_device,
        mesh=mesh,
        in_specs=placed,
        out_specs=P(("groups", "seq"), "chan"),
        check_vma=False,
    )
```

```python
import functools

import jax
import jax.numpy as jnp
from jax import lax
from jax.experimental import pallas as pl
from jax.experimental.pallas import tpu as pltpu
from jax.sharding import PartitionSpec as P

GROUP = 16
BANDS = 16
FILTERS_PER_STEP = 8
CHUNKS = 2


def filter_table(positions, total, filter_in, filter_bias, filter_out, decay):
    bands = 2.8 * 0.7 ** jnp.arange(BANDS, dtype=jnp.float32)
    angles = positions[:, None] * bands[None, :]
    feats = jnp.concatenate(
        [(positions / total)[:, None], jnp.cos(angles), jnp.sin(angles)], axis=1
    )
    hidden = jnp.sin(
        10.0 * (jnp.dot(feats, filter_in, precision=lax.Precision.HIGHEST) + filter_bias[None, :])
    )
    raw = jnp.dot(hidden, filter_out, precision=lax.Precision.HIGHEST)
    envelope = jnp.sqrt(2.0 * decay)[None, :] * jnp.exp(-decay[None, :] * positions[:, None])
    return (raw * envelope).astype(jnp.bfloat16)


def toeplitz_kernel(filt_ref, x_ref, o_ref, acc_ref):
    nb = x_ref.shape[1] // GROUP
    fb = x_ref.shape[0]
    block = x_ref.shape[2]
    upper = (lax.broadcasted_iota(jnp.int32, (block, block), 1)
             >= lax.broadcasted_iota(jnp.int32, (block, block), 0))
    for g in range(fb):
        acc_ref[...] = jnp.zeros(acc_ref.shape, jnp.float32)
        prev = None
        for d in range(nb):
            w = filt_ref[d + 1, pl.ds(g, block, stride=0), :]
            cur = pltpu.roll(w, 0, 1, stride=1, stride_axis=0)
            low = 0.0 if prev is None else prev
            t = jnp.where(upper, cur, low).astype(jnp.bfloat16)
            rows = (nb - d) * GROUP
            acc_ref[d * GROUP:, :] += jnp.dot(
                x_ref[g, :rows, :], t, preferred_element_type=jnp.float32
            )
            prev = cur
        for i in range(nb):
            o_ref[i, g * GROUP:(g + 1) * GROUP, :] = (
                acc_ref[i * GROUP:(i + 1) * GROUP, :].astype(jnp.bfloat16))


def toeplitz_conv(filt, x):
    count, rows, block = x.shape
    nb = rows // GROUP
    fb = min(FILTERS_PER_STEP, count)
    return pl.pallas_call(
        toeplitz_kernel,
        out_shape=jax.ShapeDtypeStruct((nb, count * GROUP, block), jnp.bfloat16),
        grid=(count // fb,),
        in_specs=[
            pl.BlockSpec((nb + 1, fb, block), lambda i: (0, i, 0)),
            pl.BlockSpec((fb, rows, block), lambda i: (i, 0, 0)),
        ],
        out_specs=pl.BlockSpec((nb, fb * GROUP, block), lambda i: (0, i, 0)),
        scratch_shapes=[pltpu.VMEM((rows, block), jnp.float32)],
    )(filt, x)


def exchange(x, nb, s):
    got = [x[s]]
    for k in range(1, nb):
        piece = lax.dynamic_index_in_dim(x, (s + k) % nb, 0, keepdims=False)
        got.append(lax.ppermute(piece, "seq", [(i, (i + k) % nb) for i in range(nb)]))
    z = jnp.stack(got)
    order = (s - jnp.arange(nb, dtype=jnp.int32)) % nb
    return jnp.take(z, order, axis=0)


def per_device(
    outer_gate, inner_gate, signal, filter_in, filter_bias, filter_out, decay, skip_gain
):
    own_rows, width = signal.shape
    nb = lax.axis_size("seq")
    total_rows = own_rows * nb
    s = lax.axis_index("seq")
    count = width // GROUP
    sub = count // nb
    gated = (inner_gate.astype(jnp.float32) * signal.astype(jnp.float32)).astype(jnp.bfloat16)
    gated_t = gated.T.reshape(nb, sub, GROUP, own_rows)
    positions = jnp.arange(total_rows, dtype=jnp.int32).astype(jnp.float32)
    my_out = lax.dynamic_slice_in_dim(filter_out, s * sub, sub, 1)
    my_decay = lax.dynamic_slice_in_dim(decay, s * sub, sub, 0)
    filters = filter_table(positions, float(total_rows), filter_in, filter_bias, my_out, my_decay)
    lagged = filters.astype(jnp.float32).reshape(nb, own_rows, sub).transpose(0, 2, 1)
    filt = jnp.concatenate([jnp.zeros((1, sub, own_rows), jnp.float32), lagged], axis=0)
    chunks = CHUNKS if sub % CHUNKS == 0 else 1
    part = sub // chunks
    backs = []
    for c in range(chunks):
        cut = slice(c * part, (c + 1) * part)
        got = exchange(gated_t[:, cut], nb, s)
        x = got.transpose(1, 0, 2, 3).reshape(part, nb * GROUP, own_rows)
        conv_parts = toeplitz_conv(filt[:, cut], x)
        backs.append(exchange(conv_parts, nb, s).reshape(nb, 1, part * GROUP, own_rows))
    back = jnp.concatenate(backs, axis=1)
    conv = back.reshape(width, own_rows).T.astype(jnp.float32)
    mixed = outer_gate.astype(jnp.float32) * (conv + skip_gain[None, :] * gated.astype(jnp.float32))
    return mixed.astype(jnp.bfloat16)


def solution(mesh):
    placed = (
        P(("groups", "seq"), "chan"),
        P(("groups", "seq"), "chan"),
        P(("groups", "seq"), "chan"),
        P(),
        P(),
        P(None, "chan"),
        P("chan"),
        P("chan"),
    )
    return jax.shard_map(
        per_device,
        mesh=mesh,
        in_specs=placed,
        out_specs=P(("groups", "seq"), "chan"),
        check_vma=False,
    )
```

```python
import functools

import jax
import jax.numpy as jnp
from jax import lax
from jax.experimental import pallas as pl
from jax.experimental.pallas import tpu as pltpu
from jax.sharding import PartitionSpec as P

GROUP = 16
BANDS = 16
FILTERS_PER_STEP = 8


def filter_table(positions, total, filter_in, filter_bias, filter_out, decay):
    bands = 2.8 * 0.7 ** jnp.arange(BANDS, dtype=jnp.float32)
    angles = positions[:, None] * bands[None, :]
    feats = jnp.concatenate(
        [(positions / total)[:, None], jnp.cos(angles), jnp.sin(angles)], axis=1
    )
    hidden = jnp.sin(
        10.0 * (jnp.dot(feats, filter_in, precision=lax.Precision.HIGHEST) + filter_bias[None, :])
    )
    raw = jnp.dot(hidden, filter_out, precision=lax.Precision.HIGHEST)
    envelope = jnp.sqrt(2.0 * decay)[None, :] * jnp.exp(-decay[None, :] * positions[:, None])
    return (raw * envelope).astype(jnp.bfloat16)


def toeplitz_kernel(s_ref, filt_ref, z_ref, o_ref, x_ref, acc_ref):
    nb = z_ref.shape[0]
    fb = filt_ref.shape[1]
    block = z_ref.shape[2]
    s = s_ref[0]
    upper = (lax.broadcasted_iota(jnp.int32, (block, block), 1)
             >= lax.broadcasted_iota(jnp.int32, (block, block), 0))
    for g in range(fb):
        ch = slice(g * GROUP, (g + 1) * GROUP)
        for j in range(nb):
            x_ref[j * GROUP:(j + 1) * GROUP, :] = z_ref[(s - j + nb) % nb, ch, :]
        acc_ref[...] = jnp.zeros(acc_ref.shape, jnp.float32)
        prev = None
        for d in range(nb):
            w = filt_ref[d + 1, pl.ds(g, block, stride=0), :]
            cur = pltpu.roll(w, 0, 1, stride=1, stride_axis=0)
            low = 0.0 if prev is None else prev
            t = jnp.where(upper, cur, low).astype(jnp.bfloat16)
            rows = (nb - d) * GROUP
            acc_ref[d * GROUP:, :] += jnp.dot(
                x_ref[:rows, :], t, preferred_element_type=jnp.float32
            )
            prev = cur
        for i in range(nb):
            o_ref[(i - s + nb) % nb, ch, :] = (
                acc_ref[i * GROUP:(i + 1) * GROUP, :].astype(jnp.bfloat16))


def toeplitz_conv(s, filt, z):
    nb, chans, block = z.shape
    count = chans // GROUP
    fb = min(FILTERS_PER_STEP, count)
    return pl.pallas_call(
        toeplitz_kernel,
        out_shape=jax.ShapeDtypeStruct((nb, chans, block), jnp.bfloat16),
        grid_spec=pltpu.PrefetchScalarGridSpec(
            num_scalar_prefetch=1,
            grid=(count // fb,),
            in_specs=[
                pl.BlockSpec((nb + 1, fb, block), lambda i, s_: (0, i, 0)),
                pl.BlockSpec((nb, fb * GROUP, block), lambda i, s_: (0, i, 0)),
            ],
            out_specs=pl.BlockSpec((nb, fb * GROUP, block), lambda i, s_: (0, i, 0)),
            scratch_shapes=[pltpu.VMEM((nb * GROUP, block), jnp.bfloat16),
                            pltpu.VMEM((nb * GROUP, block), jnp.float32)],
        ),
    )(s, filt, z)


def exchange(x, nb, s, ordered):
    got = [x[0] if ordered else lax.dynamic_index_in_dim(x, s, 0, keepdims=False)]
    for k in range(1, nb):
        if ordered:
            piece = x[k]
        else:
            piece = lax.dynamic_index_in_dim(x, (s + k) % nb, 0, keepdims=False)
        got.append(lax.ppermute(piece, "seq", [(i, (i + k) % nb) for i in range(nb)]))
    return jnp.stack(got)


def per_device(
    outer_gate, inner_gate, signal, filter_in, filter_bias, filter_out, decay, skip_gain
):
    own_rows, width = signal.shape
    nb = lax.axis_size("seq")
    total_rows = own_rows * nb
    s = lax.axis_index("seq")
    count = width // GROUP
    sub = count // nb
    gated = (inner_gate.astype(jnp.float32) * signal.astype(jnp.float32)).astype(jnp.bfloat16)
    gated_t = gated.T.reshape(nb, sub * GROUP, own_rows)
    got = exchange(gated_t, nb, s, False)
    positions = jnp.arange(total_rows, dtype=jnp.int32).astype(jnp.float32)
    my_out = lax.dynamic_slice_in_dim(filter_out, s * sub, sub, 1)
    my_decay = lax.dynamic_slice_in_dim(decay, s * sub, sub, 0)
    filters = filter_table(positions, float(total_rows), filter_in, filter_bias, my_out, my_decay)
    lagged = filters.astype(jnp.float32).reshape(nb, own_rows, sub).transpose(0, 2, 1)
    filt = jnp.concatenate([jnp.zeros((1, sub, own_rows), jnp.float32), lagged], axis=0)
    s_arr = jnp.reshape(s, (1,)).astype(jnp.int32)
    conv_parts = toeplitz_conv(s_arr, filt, got)
    back = exchange(conv_parts, nb, s, True)
    order = (s - jnp.arange(nb, dtype=jnp.int32) + nb) % nb
    back = jnp.take(back, order, axis=0)
    conv = back.reshape(width, own_rows).T.astype(jnp.float32)
    mixed = outer_gate.astype(jnp.float32) * (conv + skip_gain[None, :] * gated.astype(jnp.float32))
    return mixed.astype(jnp.bfloat16)


def solution(mesh):
    placed = (
        P(("groups", "seq"), "chan"),
        P(("groups", "seq"), "chan"),
        P(("groups", "seq"), "chan"),
        P(),
        P(),
        P(None, "chan"),
        P("chan"),
        P("chan"),
    )
    return jax.shard_map(
        per_device,
        mesh=mesh,
        in_specs=placed,
        out_specs=P(("groups", "seq"), "chan"),
        check_vma=False,
    )
```

```python
import functools

import jax
import jax.numpy as jnp
from jax import lax
from jax.experimental import pallas as pl
from jax.experimental.pallas import tpu as pltpu
from jax.sharding import PartitionSpec as P

GROUP = 16
BANDS = 16
FILTERS_PER_STEP = 8


def filter_table(positions, total, filter_in, filter_bias, filter_out, decay):
    bands = 2.8 * 0.7 ** jnp.arange(BANDS, dtype=jnp.float32)
    angles = positions[:, None] * bands[None, :]
    feats = jnp.concatenate(
        [(positions / total)[:, None], jnp.cos(angles), jnp.sin(angles)], axis=1
    )
    hidden = jnp.sin(
        10.0 * (jnp.dot(feats, filter_in, precision=lax.Precision.HIGHEST) + filter_bias[None, :])
    )
    raw = jnp.dot(hidden, filter_out, precision=lax.Precision.HIGHEST)
    envelope = jnp.sqrt(2.0 * decay)[None, :] * jnp.exp(-decay[None, :] * positions[:, None])
    return (raw * envelope).astype(jnp.bfloat16)


def toeplitz_kernel(s_ref, filt_ref, z_ref, o_ref, x_ref, acc_ref):
    nb = z_ref.shape[0]
    fb = filt_ref.shape[1]
    block = z_ref.shape[2]
    s = s_ref[0]
    upper = (lax.broadcasted_iota(jnp.int32, (block, block), 1)
             >= lax.broadcasted_iota(jnp.int32, (block, block), 0))
    for g in range(fb):
        ch = slice(g * GROUP, (g + 1) * GROUP)
        for j in range(nb):
            x_ref[j * GROUP:(j + 1) * GROUP, :] = z_ref[(s - j + nb) % nb, ch, :]
        acc_ref[...] = jnp.zeros(acc_ref.shape, jnp.float32)
        prev = None
        for d in range(nb):
            w = filt_ref[d + 1, pl.ds(g, block, stride=0), :]
            cur = pltpu.roll(w, 0, 1, stride=1, stride_axis=0)
            low = 0.0 if prev is None else prev
            t = jnp.where(upper, cur, low).astype(jnp.bfloat16)
            rows = (nb - d) * GROUP
            acc_ref[d * GROUP:, :] += jnp.dot(
                x_ref[:rows, :], t, preferred_element_type=jnp.float32
            )
            prev = cur
        for i in range(nb):
            o_ref[(i - s + nb) % nb, ch, :] = (
                acc_ref[i * GROUP:(i + 1) * GROUP, :].astype(jnp.bfloat16))


def toeplitz_conv(s, filt, z):
    nb, chans, block = z.shape
    count = chans // GROUP
    fb = min(FILTERS_PER_STEP, count)
    return pl.pallas_call(
        toeplitz_kernel,
        out_shape=jax.ShapeDtypeStruct((nb, chans, block), jnp.bfloat16),
        grid_spec=pltpu.PrefetchScalarGridSpec(
            num_scalar_prefetch=1,
            grid=(count // fb,),
            in_specs=[
                pl.BlockSpec((nb + 1, fb, block), lambda i, s_: (0, i, 0)),
                pl.BlockSpec((nb, fb * GROUP, block), lambda i, s_: (0, i, 0)),
            ],
            out_specs=pl.BlockSpec((nb, fb * GROUP, block), lambda i, s_: (0, i, 0)),
            scratch_shapes=[pltpu.VMEM((nb * GROUP, block), jnp.bfloat16),
                            pltpu.VMEM((nb * GROUP, block), jnp.float32)],
        ),
    )(s, filt, z)


def exchange(x, nb, s, ordered):
    got = [x[0] if ordered else lax.dynamic_index_in_dim(x, s, 0, keepdims=False)]
    for k in range(1, nb):
        if ordered:
            piece = x[k]
        else:
            piece = lax.dynamic_index_in_dim(x, (s + k) % nb, 0, keepdims=False)
        got.append(lax.ppermute(piece, "seq", [(i, (i + k) % nb) for i in range(nb)]))
    return jnp.stack(got)


def per_device(
    outer_gate, inner_gate, signal, filter_in, filter_bias, filter_out, decay, skip_gain
):
    own_rows, width = signal.shape
    nb = lax.axis_size("seq")
    total_rows = own_rows * nb
    s = lax.axis_index("seq")
    count = width // GROUP
    sub = count // nb
    gated_f = lax.reduce_precision(
        inner_gate.astype(jnp.float32) * signal.astype(jnp.float32), exponent_bits=8, mantissa_bits=7)
    gated = gated_f.astype(jnp.bfloat16)
    gated_t = gated.T.reshape(nb, sub * GROUP, own_rows)
    got = exchange(gated_t, nb, s, False)
    positions = jnp.arange(total_rows, dtype=jnp.int32).astype(jnp.float32)
    my_out = lax.dynamic_slice_in_dim(filter_out, s * sub, sub, 1)
    my_decay = lax.dynamic_slice_in_dim(decay, s * sub, sub, 0)
    filters = filter_table(positions, float(total_rows), filter_in, filter_bias, my_out, my_decay)
    lagged = filters.astype(jnp.float32).reshape(nb, own_rows, sub).transpose(0, 2, 1)
    filt = jnp.concatenate([jnp.zeros((1, sub, own_rows), jnp.float32), lagged], axis=0)
    s_arr = jnp.reshape(s, (1,)).astype(jnp.int32)
    conv_parts = toeplitz_conv(s_arr, filt, got)
    back = exchange(conv_parts, nb, s, True)
    order = (s - jnp.arange(nb, dtype=jnp.int32) + nb) % nb
    back = jnp.take(back, order, axis=0)
    conv = back.reshape(width, own_rows).T.astype(jnp.float32)
    mixed = outer_gate.astype(jnp.float32) * (conv + skip_gain[None, :] * gated_f)
    return mixed.astype(jnp.bfloat16)


def solution(mesh):
    placed = (
        P(("groups", "seq"), "chan"),
        P(("groups", "seq"), "chan"),
        P(("groups", "seq"), "chan"),
        P(),
        P(),
        P(None, "chan"),
        P("chan"),
        P("chan"),
    )
    return jax.shard_map(
        per_device,
        mesh=mesh,
        in_specs=placed,
        out_specs=P(("groups", "seq"), "chan"),
        check_vma=False,
    )
```

```python
import functools

import jax
import jax.numpy as jnp
from jax import lax
from jax.experimental import pallas as pl
from jax.experimental.pallas import tpu as pltpu
from jax.sharding import PartitionSpec as P

GROUP = 16
BANDS = 16
FILTERS_PER_STEP = 8


def filter_table(positions, total, filter_in, filter_bias, filter_out, decay):
    bands = 2.8 * 0.7 ** jnp.arange(BANDS, dtype=jnp.float32)
    angles = positions[:, None] * bands[None, :]
    feats = jnp.concatenate(
        [(positions / total)[:, None], jnp.cos(angles), jnp.sin(angles)], axis=1
    )
    hidden = jnp.sin(
        10.0 * (jnp.dot(feats, filter_in, precision=lax.Precision.HIGHEST) + filter_bias[None, :])
    )
    raw = jnp.dot(hidden, filter_out, precision=lax.Precision.HIGHEST)
    envelope = jnp.sqrt(2.0 * decay)[None, :] * jnp.exp(-decay[None, :] * positions[:, None])
    return (raw * envelope).astype(jnp.bfloat16)


def toeplitz_kernel(s_ref, filt_ref, *refs):
    nb = filt_ref.shape[0] - 1
    z_refs, o_refs = refs[:nb], refs[nb:2 * nb]
    x_ref, acc_ref = refs[2 * nb:]
    fb = filt_ref.shape[1]
    block = filt_ref.shape[2]
    s = s_ref[0]
    upper = (lax.broadcasted_iota(jnp.int32, (block, block), 1)
             >= lax.broadcasted_iota(jnp.int32, (block, block), 0))
    for g in range(fb):
        ch = slice(g * GROUP, (g + 1) * GROUP)
        for k in range(nb):
            j = (s - k + nb) % nb
            x_ref[pl.ds(pl.multiple_of(j * GROUP, GROUP), GROUP), :] = z_refs[k][ch, :]
        acc_ref[...] = jnp.zeros(acc_ref.shape, jnp.float32)
        prev = None
        for d in range(nb):
            w = filt_ref[d + 1, pl.ds(g, block, stride=0), :]
            cur = pltpu.roll(w, 0, 1, stride=1, stride_axis=0)
            low = 0.0 if prev is None else prev
            t = jnp.where(upper, cur, low).astype(jnp.bfloat16)
            rows = (nb - d) * GROUP
            acc_ref[d * GROUP:, :] += jnp.dot(
                x_ref[:rows, :], t, preferred_element_type=jnp.float32
            )
            prev = cur
        for k in range(nb):
            i = (s + k) % nb
            o_refs[k][ch, :] = acc_ref[pl.ds(pl.multiple_of(i * GROUP, GROUP), GROUP), :].astype(
                jnp.bfloat16)


def toeplitz_conv(s, filt, pieces):
    nb = len(pieces)
    chans, block = pieces[0].shape
    count = chans // GROUP
    fb = min(FILTERS_PER_STEP, count)
    piece_spec = pl.BlockSpec((fb * GROUP, block), lambda i, s_: (i, 0))
    return pl.pallas_call(
        toeplitz_kernel,
        out_shape=[jax.ShapeDtypeStruct((chans, block), jnp.bfloat16) for _ in range(nb)],
        grid_spec=pltpu.PrefetchScalarGridSpec(
            num_scalar_prefetch=1,
            grid=(count // fb,),
            in_specs=[pl.BlockSpec((nb + 1, fb, block), lambda i, s_: (0, i, 0))]
            + [piece_spec] * nb,
            out_specs=[piece_spec] * nb,
            scratch_shapes=[pltpu.VMEM((nb * GROUP, block), jnp.bfloat16),
                            pltpu.VMEM((nb * GROUP, block), jnp.float32)],
        ),
    )(s, filt, *pieces)


def exchange(pieces, nb):
    got = [pieces[0]]
    for k in range(1, nb):
        got.append(lax.ppermute(pieces[k], "seq", [(i, (i + k) % nb) for i in range(nb)]))
    return got


def per_device(
    outer_gate, inner_gate, signal, filter_in, filter_bias, filter_out, decay, skip_gain
):
    own_rows, width = signal.shape
    nb = lax.axis_size("seq")
    total_rows = own_rows * nb
    s = lax.axis_index("seq")
    count = width // GROUP
    sub = count // nb
    gated_f = lax.reduce_precision(
        inner_gate.astype(jnp.float32) * signal.astype(jnp.float32), exponent_bits=8, mantissa_bits=7)
    gated = gated_f.astype(jnp.bfloat16)
    gated_t = gated.T.reshape(nb, sub * GROUP, own_rows)
    got = exchange(
        [lax.dynamic_index_in_dim(gated_t, (s + k) % nb, 0, keepdims=False) for k in range(nb)], nb)
    positions = jnp.arange(total_rows, dtype=jnp.int32).astype(jnp.float32)
    my_out = lax.dynamic_slice_in_dim(filter_out, s * sub, sub, 1)
    my_decay = lax.dynamic_slice_in_dim(decay, s * sub, sub, 0)
    filters = filter_table(positions, float(total_rows), filter_in, filter_bias, my_out, my_decay)
    lagged = filters.astype(jnp.float32).reshape(nb, own_rows, sub).transpose(0, 2, 1)
    filt = jnp.concatenate([jnp.zeros((1, sub, own_rows), jnp.float32), lagged], axis=0)
    s_arr = jnp.reshape(s, (1,)).astype(jnp.int32)
    conv_parts = toeplitz_conv(s_arr, filt, got)
    back = jnp.stack(exchange(conv_parts, nb))
    order = (s - jnp.arange(nb, dtype=jnp.int32) + nb) % nb
    back = jnp.take(back, order, axis=0)
    conv = back.reshape(width, own_rows).T.astype(jnp.float32)
    mixed = outer_gate.astype(jnp.float32) * (conv + skip_gain[None, :] * gated_f)
    return mixed.astype(jnp.bfloat16)


def solution(mesh):
    placed = (
        P(("groups", "seq"), "chan"),
        P(("groups", "seq"), "chan"),
        P(("groups", "seq"), "chan"),
        P(),
        P(),
        P(None, "chan"),
        P("chan"),
        P("chan"),
    )
    return jax.shard_map(
        per_device,
        mesh=mesh,
        in_specs=placed,
        out_specs=P(("groups", "seq"), "chan"),
        check_vma=False,
    )
```

```python
import functools

import jax
import jax.numpy as jnp
from jax import lax
from jax.experimental import pallas as pl
from jax.experimental.pallas import tpu as pltpu
from jax.sharding import PartitionSpec as P

GROUP = 16
BANDS = 16
FILTERS_PER_STEP = 16


def filter_table(positions, total, filter_in, filter_bias, filter_out, decay):
    bands = 2.8 * 0.7 ** jnp.arange(BANDS, dtype=jnp.float32)
    angles = positions[:, None] * bands[None, :]
    feats = jnp.concatenate(
        [(positions / total)[:, None], jnp.cos(angles), jnp.sin(angles)], axis=1
    )
    hidden = jnp.sin(
        10.0 * (jnp.dot(feats, filter_in, precision=lax.Precision.HIGHEST) + filter_bias[None, :])
    )
    raw = jnp.dot(hidden, filter_out, precision=lax.Precision.HIGHEST)
    envelope = jnp.sqrt(2.0 * decay)[None, :] * jnp.exp(-decay[None, :] * positions[:, None])
    return (raw * envelope).astype(jnp.bfloat16)


def toeplitz_kernel(s_ref, filt_ref, z_ref, o_ref, x_ref, acc_ref):
    nb = z_ref.shape[0]
    fb = filt_ref.shape[1]
    block = z_ref.shape[2]
    s = s_ref[0]
    upper = (lax.broadcasted_iota(jnp.int32, (block, block), 1)
             >= lax.broadcasted_iota(jnp.int32, (block, block), 0))
    for g in range(fb):
        ch = slice(g * GROUP, (g + 1) * GROUP)
        for j in range(nb):
            x_ref[j * GROUP:(j + 1) * GROUP, :] = z_ref[(s - j + nb) % nb, ch, :]
        acc_ref[...] = jnp.zeros(acc_ref.shape, jnp.float32)
        prev = None
        for d in range(nb):
            w = filt_ref[d + 1, pl.ds(g, block, stride=0), :]
            cur = pltpu.roll(w, 0, 1, stride=1, stride_axis=0)
            low = 0.0 if prev is None else prev
            t = jnp.where(upper, cur, low).astype(jnp.bfloat16)
            rows = (nb - d) * GROUP
            acc_ref[d * GROUP:, :] += jnp.dot(
                x_ref[:rows, :], t, preferred_element_type=jnp.float32
            )
            prev = cur
        for i in range(nb):
            o_ref[(i - s + nb) % nb, ch, :] = (
                acc_ref[i * GROUP:(i + 1) * GROUP, :].astype(jnp.bfloat16))


def toeplitz_conv(s, filt, z):
    nb, chans, block = z.shape
    count = chans // GROUP
    fb = min(FILTERS_PER_STEP, count)
    return pl.pallas_call(
        toeplitz_kernel,
        out_shape=jax.ShapeDtypeStruct((nb, chans, block), jnp.bfloat16),
        grid_spec=pltpu.PrefetchScalarGridSpec(
            num_scalar_prefetch=1,
            grid=(count // fb,),
            in_specs=[
                pl.BlockSpec((nb + 1, fb, block), lambda i, s_: (0, i, 0)),
                pl.BlockSpec((nb, fb * GROUP, block), lambda i, s_: (0, i, 0)),
            ],
            out_specs=pl.BlockSpec((nb, fb * GROUP, block), lambda i, s_: (0, i, 0)),
            scratch_shapes=[pltpu.VMEM((nb * GROUP, block), jnp.bfloat16),
                            pltpu.VMEM((nb * GROUP, block), jnp.float32)],
        ),
    )(s, filt, z)


def exchange(x, nb, s, ordered):
    got = [x[0] if ordered else lax.dynamic_index_in_dim(x, s, 0, keepdims=False)]
    for k in range(1, nb):
        if ordered:
            piece = x[k]
        else:
            piece = lax.dynamic_index_in_dim(x, (s + k) % nb, 0, keepdims=False)
        got.append(lax.ppermute(piece, "seq", [(i, (i + k) % nb) for i in range(nb)]))
    return jnp.stack(got)


def per_device(
    outer_gate, inner_gate, signal, filter_in, filter_bias, filter_out, decay, skip_gain
):
    own_rows, width = signal.shape
    nb = lax.axis_size("seq")
    total_rows = own_rows * nb
    s = lax.axis_index("seq")
    count = width // GROUP
    sub = count // nb
    gated_f = lax.reduce_precision(
        inner_gate.astype(jnp.float32) * signal.astype(jnp.float32), exponent_bits=8, mantissa_bits=7)
    gated = gated_f.astype(jnp.bfloat16)
    gated_t = gated.T.reshape(nb, sub * GROUP, own_rows)
    got = exchange(gated_t, nb, s, False)
    positions = jnp.arange(total_rows, dtype=jnp.int32).astype(jnp.float32)
    my_out = lax.dynamic_slice_in_dim(filter_out, s * sub, sub, 1)
    my_decay = lax.dynamic_slice_in_dim(decay, s * sub, sub, 0)
    filters = filter_table(positions, float(total_rows), filter_in, filter_bias, my_out, my_decay)
    lagged = filters.astype(jnp.float32).reshape(nb, own_rows, sub).transpose(0, 2, 1)
    filt = jnp.concatenate([jnp.zeros((1, sub, own_rows), jnp.float32), lagged], axis=0)
    s_arr = jnp.reshape(s, (1,)).astype(jnp.int32)
    conv_parts = toeplitz_conv(s_arr, filt, got)
    back = exchange(conv_parts, nb, s, True)
    order = (s - jnp.arange(nb, dtype=jnp.int32) + nb) % nb
    back = jnp.take(back, order, axis=0)
    conv = back.reshape(width, own_rows).T.astype(jnp.float32)
    mixed = outer_gate.astype(jnp.float32) * (conv + skip_gain[None, :] * gated_f)
    return mixed.astype(jnp.bfloat16)


def solution(mesh):
    placed = (
        P(("groups", "seq"), "chan"),
        P(("groups", "seq"), "chan"),
        P(("groups", "seq"), "chan"),
        P(),
        P(),
        P(None, "chan"),
        P("chan"),
        P("chan"),
    )
    return jax.shard_map(
        per_device,
        mesh=mesh,
        in_specs=placed,
        out_specs=P(("groups", "seq"), "chan"),
        check_vma=False,
    )
```

```python
import functools

import jax
import jax.numpy as jnp
from jax import lax
from jax.experimental import pallas as pl
from jax.experimental.pallas import tpu as pltpu
from jax.sharding import PartitionSpec as P

GROUP = 16
BANDS = 16
FILTERS_PER_STEP = 32


def filter_table(positions, total, filter_in, filter_bias, filter_out, decay):
    bands = 2.8 * 0.7 ** jnp.arange(BANDS, dtype=jnp.float32)
    angles = positions[:, None] * bands[None, :]
    feats = jnp.concatenate(
        [(positions / total)[:, None], jnp.cos(angles), jnp.sin(angles)], axis=1
    )
    hidden = jnp.sin(
        10.0 * (jnp.dot(feats, filter_in, precision=lax.Precision.HIGHEST) + filter_bias[None, :])
    )
    raw = jnp.dot(hidden, filter_out, precision=lax.Precision.HIGHEST)
    envelope = jnp.sqrt(2.0 * decay)[None, :] * jnp.exp(-decay[None, :] * positions[:, None])
    return (raw * envelope).astype(jnp.bfloat16)


def toeplitz_kernel(s_ref, filt_ref, z_ref, o_ref, x_ref, acc_ref):
    nb = z_ref.shape[0]
    fb = filt_ref.shape[1]
    block = z_ref.shape[2]
    s = s_ref[0]
    upper = (lax.broadcasted_iota(jnp.int32, (block, block), 1)
             >= lax.broadcasted_iota(jnp.int32, (block, block), 0))
    for g in range(fb):
        ch = slice(g * GROUP, (g + 1) * GROUP)
        for j in range(nb):
            x_ref[j * GROUP:(j + 1) * GROUP, :] = z_ref[(s - j + nb) % nb, ch, :]
        acc_ref[...] = jnp.zeros(acc_ref.shape, jnp.float32)
        prev = None
        for d in range(nb):
            w = filt_ref[d + 1, pl.ds(g, block, stride=0), :]
            cur = pltpu.roll(w, 0, 1, stride=1, stride_axis=0)
            low = 0.0 if prev is None else prev
            t = jnp.where(upper, cur, low).astype(jnp.bfloat16)
            rows = (nb - d) * GROUP
            acc_ref[d * GROUP:, :] += jnp.dot(
                x_ref[:rows, :], t, preferred_element_type=jnp.float32
            )
            prev = cur
        for i in range(nb):
            o_ref[(i - s + nb) % nb, ch, :] = (
                acc_ref[i * GROUP:(i + 1) * GROUP, :].astype(jnp.bfloat16))


def toeplitz_conv(s, filt, z):
    nb, chans, block = z.shape
    count = chans // GROUP
    fb = min(FILTERS_PER_STEP, count)
    return pl.pallas_call(
        toeplitz_kernel,
        out_shape=jax.ShapeDtypeStruct((nb, chans, block), jnp.bfloat16),
        grid_spec=pltpu.PrefetchScalarGridSpec(
            num_scalar_prefetch=1,
            grid=(count // fb,),
            in_specs=[
                pl.BlockSpec((nb + 1, fb, block), lambda i, s_: (0, i, 0)),
                pl.BlockSpec((nb, fb * GROUP, block), lambda i, s_: (0, i, 0)),
            ],
            out_specs=pl.BlockSpec((nb, fb * GROUP, block), lambda i, s_: (0, i, 0)),
            scratch_shapes=[pltpu.VMEM((nb * GROUP, block), jnp.bfloat16),
                            pltpu.VMEM((nb * GROUP, block), jnp.float32)],
        ),
    )(s, filt, z)


def exchange(x, nb, s, ordered):
    got = [x[0] if ordered else lax.dynamic_index_in_dim(x, s, 0, keepdims=False)]
    for k in range(1, nb):
        if ordered:
            piece = x[k]
        else:
            piece = lax.dynamic_index_in_dim(x, (s + k) % nb, 0, keepdims=False)
        got.append(lax.ppermute(piece, "seq", [(i, (i + k) % nb) for i in range(nb)]))
    return jnp.stack(got)


def per_device(
    outer_gate, inner_gate, signal, filter_in, filter_bias, filter_out, decay, skip_gain
):
    own_rows, width = signal.shape
    nb = lax.axis_size("seq")
    total_rows = own_rows * nb
    s = lax.axis_index("seq")
    count = width // GROUP
    sub = count // nb
    gated_f = lax.reduce_precision(
        inner_gate.astype(jnp.float32) * signal.astype(jnp.float32), exponent_bits=8, mantissa_bits=7)
    gated = gated_f.astype(jnp.bfloat16)
    gated_t = gated.T.reshape(nb, sub * GROUP, own_rows)
    got = exchange(gated_t, nb, s, False)
    positions = jnp.arange(total_rows, dtype=jnp.int32).astype(jnp.float32)
    my_out = lax.dynamic_slice_in_dim(filter_out, s * sub, sub, 1)
    my_decay = lax.dynamic_slice_in_dim(decay, s * sub, sub, 0)
    filters = filter_table(positions, float(total_rows), filter_in, filter_bias, my_out, my_decay)
    lagged = filters.astype(jnp.float32).reshape(nb, own_rows, sub).transpose(0, 2, 1)
    filt = jnp.concatenate([jnp.zeros((1, sub, own_rows), jnp.float32), lagged], axis=0)
    s_arr = jnp.reshape(s, (1,)).astype(jnp.int32)
    conv_parts = toeplitz_conv(s_arr, filt, got)
    back = exchange(conv_parts, nb, s, True)
    order = (s - jnp.arange(nb, dtype=jnp.int32) + nb) % nb
    back = jnp.take(back, order, axis=0)
    conv = back.reshape(width, own_rows).T.astype(jnp.float32)
    mixed = outer_gate.astype(jnp.float32) * (conv + skip_gain[None, :] * gated_f)
    return mixed.astype(jnp.bfloat16)


def solution(mesh):
    placed = (
        P(("groups", "seq"), "chan"),
        P(("groups", "seq"), "chan"),
        P(("groups", "seq"), "chan"),
        P(),
        P(),
        P(None, "chan"),
        P("chan"),
        P("chan"),
    )
    return jax.shard_map(
        per_device,
        mesh=mesh,
        in_specs=placed,
        out_specs=P(("groups", "seq"), "chan"),
        check_vma=False,
    )
```

```python
import functools

import jax
import jax.numpy as jnp
from jax import lax
from jax.experimental import pallas as pl
from jax.experimental.pallas import tpu as pltpu
from jax.sharding import PartitionSpec as P

GROUP = 16
BANDS = 16
FILTERS_PER_STEP = 16


def filter_table(positions, total, filter_in, filter_bias, filter_out, decay):
    bands = 2.8 * 0.7 ** jnp.arange(BANDS, dtype=jnp.float32)
    angles = positions[:, None] * bands[None, :]
    feats = jnp.concatenate(
        [(positions / total)[:, None], jnp.cos(angles), jnp.sin(angles)], axis=1
    )
    hidden = jnp.sin(
        10.0 * (jnp.dot(feats, filter_in, precision=lax.Precision.HIGHEST) + filter_bias[None, :])
    )
    raw = jnp.dot(hidden, filter_out, precision=lax.Precision.HIGHEST)
    envelope = jnp.sqrt(2.0 * decay)[None, :] * jnp.exp(-decay[None, :] * positions[:, None])
    return (raw * envelope).astype(jnp.bfloat16)


def toeplitz_kernel(s_ref, filt_ref, z_ref, o_ref, x_ref, acc_ref):
    nb = z_ref.shape[0]
    fb = filt_ref.shape[1]
    block = z_ref.shape[2]
    s = s_ref[0]
    upper = (lax.broadcasted_iota(jnp.int32, (block, block), 1)
             >= lax.broadcasted_iota(jnp.int32, (block, block), 0))
    for g in range(fb):
        ch = slice(g * GROUP, (g + 1) * GROUP)
        for j in range(nb):
            x_ref[j * GROUP:(j + 1) * GROUP, :] = z_ref[(s - j + nb) % nb, ch, :]
        acc_ref[...] = jnp.zeros(acc_ref.shape, jnp.float32)
        prev = None
        for d in range(nb):
            w = filt_ref[d + 1, pl.ds(g, block, stride=0), :]
            cur = pltpu.roll(w, 0, 1, stride=1, stride_axis=0)
            low = 0.0 if prev is None else prev
            t = jnp.where(upper, cur, low).astype(jnp.bfloat16)
            rows = (nb - d) * GROUP
            acc_ref[d * GROUP:, :] += jnp.dot(
                x_ref[:rows, :], t, preferred_element_type=jnp.float32
            )
            prev = cur
        for i in range(nb):
            o_ref[(i - s + nb) % nb, ch, :] = (
                acc_ref[i * GROUP:(i + 1) * GROUP, :].astype(jnp.bfloat16))


def toeplitz_conv(s, filt, z):
    nb, chans, block = z.shape
    count = chans // GROUP
    fb = min(FILTERS_PER_STEP, count)
    return pl.pallas_call(
        toeplitz_kernel,
        out_shape=jax.ShapeDtypeStruct((nb, chans, block), jnp.bfloat16),
        grid_spec=pltpu.PrefetchScalarGridSpec(
            num_scalar_prefetch=1,
            grid=(count // fb,),
            in_specs=[
                pl.BlockSpec((nb + 1, fb, block), lambda i, s_: (0, i, 0)),
                pl.BlockSpec((nb, fb * GROUP, block), lambda i, s_: (0, i, 0)),
            ],
            out_specs=pl.BlockSpec((nb, fb * GROUP, block), lambda i, s_: (0, i, 0)),
            scratch_shapes=[pltpu.VMEM((nb * GROUP, block), jnp.bfloat16),
                            pltpu.VMEM((nb * GROUP, block), jnp.float32)],
        ),
    )(s, filt, z)


def exchange(x, nb, s, ordered):
    got = [x[0] if ordered else lax.dynamic_index_in_dim(x, s, 0, keepdims=False)]
    for k in range(1, nb):
        if ordered:
            piece = x[k]
        else:
            piece = lax.dynamic_index_in_dim(x, (s + k) % nb, 0, keepdims=False)
        got.append(lax.ppermute(piece, "seq", [(i, (i + k) % nb) for i in range(nb)]))
    return jnp.stack(got)


def mix_kernel(s_ref, z_ref, outer_ref, inner_ref, signal_ref, skip_ref, o_ref):
    conv = z_ref[0].astype(jnp.float32).T
    gated = (inner_ref[...].astype(jnp.float32) * signal_ref[...].astype(jnp.float32)).astype(
        jnp.bfloat16).astype(jnp.float32)
    o_ref[...] = (outer_ref[...].astype(jnp.float32) * (conv + skip_ref[...] * gated)).astype(
        jnp.bfloat16)


def mix(s, back, outer_gate, inner_gate, signal, skip_gain):
    nb, chunk, block = back.shape

    def cols(k, s_):
        return (0, (s_[0] - k + nb) % nb)

    row_spec = pl.BlockSpec((block, chunk), cols)
    return pl.pallas_call(
        mix_kernel,
        out_shape=jax.ShapeDtypeStruct(outer_gate.shape, jnp.bfloat16),
        grid_spec=pltpu.PrefetchScalarGridSpec(
            num_scalar_prefetch=1,
            grid=(nb,),
            in_specs=[
                pl.BlockSpec((1, chunk, block), lambda k, s_: (k, 0, 0)),
                row_spec, row_spec, row_spec,
                pl.BlockSpec((1, chunk), cols),
            ],
            out_specs=row_spec,
        ),
    )(s, back, outer_gate, inner_gate, signal, skip_gain[None, :])


def per_device(
    outer_gate, inner_gate, signal, filter_in, filter_bias, filter_out, decay, skip_gain
):
    own_rows, width = signal.shape
    nb = lax.axis_size("seq")
    total_rows = own_rows * nb
    s = lax.axis_index("seq")
    count = width // GROUP
    sub = count // nb
    gated_f = lax.reduce_precision(
        inner_gate.astype(jnp.float32) * signal.astype(jnp.float32), exponent_bits=8, mantissa_bits=7)
    gated = gated_f.astype(jnp.bfloat16)
    gated_t = gated.T.reshape(nb, sub * GROUP, own_rows)
    got = exchange(gated_t, nb, s, False)
    positions = jnp.arange(total_rows, dtype=jnp.int32).astype(jnp.float32)
    my_out = lax.dynamic_slice_in_dim(filter_out, s * sub, sub, 1)
    my_decay = lax.dynamic_slice_in_dim(decay, s * sub, sub, 0)
    filters = filter_table(positions, float(total_rows), filter_in, filter_bias, my_out, my_decay)
    lagged = filters.astype(jnp.float32).reshape(nb, own_rows, sub).transpose(0, 2, 1)
    filt = jnp.concatenate([jnp.zeros((1, sub, own_rows), jnp.float32), lagged], axis=0)
    s_arr = jnp.reshape(s, (1,)).astype(jnp.int32)
    conv_parts = toeplitz_conv(s_arr, filt, got)
    back = exchange(conv_parts, nb, s, True)
    if (sub * GROUP) % 128 == 0:
        return mix(s_arr, back, outer_gate, inner_gate, signal, skip_gain)
    order = (s - jnp.arange(nb, dtype=jnp.int32) + nb) % nb
    back = jnp.take(back, order, axis=0)
    conv = back.reshape(width, own_rows).T.astype(jnp.float32)
    mixed = outer_gate.astype(jnp.float32) * (conv + skip_gain[None, :] * gated_f)
    return mixed.astype(jnp.bfloat16)


def solution(mesh):
    placed = (
        P(("groups", "seq"), "chan"),
        P(("groups", "seq"), "chan"),
        P(("groups", "seq"), "chan"),
        P(),
        P(),
        P(None, "chan"),
        P("chan"),
        P("chan"),
    )
    return jax.shard_map(
        per_device,
        mesh=mesh,
        in_specs=placed,
        out_specs=P(("groups", "seq"), "chan"),
        check_vma=False,
    )
```

```python
import functools

import jax
import jax.numpy as jnp
from jax import lax
from jax.experimental import pallas as pl
from jax.experimental.pallas import tpu as pltpu
from jax.sharding import PartitionSpec as P

GROUP = 16
BANDS = 16
FILTERS_PER_STEP = 16


def filter_table(positions, total, filter_in, filter_bias, filter_out, decay):
    bands = 2.8 * 0.7 ** jnp.arange(BANDS, dtype=jnp.float32)
    angles = positions[:, None] * bands[None, :]
    feats = jnp.concatenate(
        [(positions / total)[:, None], jnp.cos(angles), jnp.sin(angles)], axis=1
    )
    hidden = jnp.sin(
        10.0 * (jnp.dot(feats, filter_in, precision=lax.Precision.HIGHEST) + filter_bias[None, :])
    )
    raw = jnp.dot(hidden, filter_out, precision=lax.Precision.HIGHEST)
    envelope = jnp.sqrt(2.0 * decay)[None, :] * jnp.exp(-decay[None, :] * positions[:, None])
    return (raw * envelope).astype(jnp.bfloat16)


def toeplitz_kernel(s_ref, filt_ref, z_ref, o_ref, x_ref, acc_ref):
    nb = z_ref.shape[0]
    fb = filt_ref.shape[1]
    block = z_ref.shape[2]
    s = s_ref[0]
    upper = (lax.broadcasted_iota(jnp.int32, (block, block), 1)
             >= lax.broadcasted_iota(jnp.int32, (block, block), 0))
    for g in range(fb):
        ch = slice(g * GROUP, (g + 1) * GROUP)
        for j in range(nb):
            x_ref[j * GROUP:(j + 1) * GROUP, :] = z_ref[source(s, j, nb), ch, :]
        acc_ref[...] = jnp.zeros(acc_ref.shape, jnp.float32)
        prev = None
        for d in range(nb):
            w = filt_ref[d + 1, pl.ds(g, block, stride=0), :]
            cur = pltpu.roll(w, 0, 1, stride=1, stride_axis=0)
            low = 0.0 if prev is None else prev
            t = jnp.where(upper, cur, low).astype(jnp.bfloat16)
            rows = (nb - d) * GROUP
            acc_ref[d * GROUP:, :] += jnp.dot(
                x_ref[:rows, :], t, preferred_element_type=jnp.float32
            )
            prev = cur
        for i in range(nb):
            o_ref[source(i, s, nb), ch, :] = (
                acc_ref[i * GROUP:(i + 1) * GROUP, :].astype(jnp.bfloat16))


def toeplitz_conv(s, filt, z):
    nb, chans, block = z.shape
    count = chans // GROUP
    fb = min(FILTERS_PER_STEP, count)
    return pl.pallas_call(
        toeplitz_kernel,
        out_shape=jax.ShapeDtypeStruct((nb, chans, block), jnp.bfloat16),
        grid_spec=pltpu.PrefetchScalarGridSpec(
            num_scalar_prefetch=1,
            grid=(count // fb,),
            in_specs=[
                pl.BlockSpec((nb + 1, fb, block), lambda i, s_: (0, i, 0)),
                pl.BlockSpec((nb, fb * GROUP, block), lambda i, s_: (0, i, 0)),
            ],
            out_specs=pl.BlockSpec((nb, fb * GROUP, block), lambda i, s_: (0, i, 0)),
            scratch_shapes=[pltpu.VMEM((nb * GROUP, block), jnp.bfloat16),
                            pltpu.VMEM((nb * GROUP, block), jnp.float32)],
        ),
    )(s, filt, z)


def partner(s, k, nb):
    if nb & (nb - 1) == 0:
        return s ^ k
    return (s + k) % nb


def source(s, k, nb):
    if nb & (nb - 1) == 0:
        return s ^ k
    return (s - k + nb) % nb


def exchange(x, nb, s, ordered):
    got = [x[0] if ordered else lax.dynamic_index_in_dim(x, s, 0, keepdims=False)]
    for k in range(1, nb):
        if ordered:
            piece = x[k]
        else:
            piece = lax.dynamic_index_in_dim(x, partner(s, k, nb), 0, keepdims=False)
        got.append(lax.ppermute(piece, "seq", [(i, partner(i, k, nb)) for i in range(nb)]))
    return jnp.stack(got)


def per_device(
    outer_gate, inner_gate, signal, filter_in, filter_bias, filter_out, decay, skip_gain
):
    own_rows, width = signal.shape
    nb = lax.axis_size("seq")
    total_rows = own_rows * nb
    s = lax.axis_index("seq")
    count = width // GROUP
    sub = count // nb
    gated_f = lax.reduce_precision(
        inner_gate.astype(jnp.float32) * signal.astype(jnp.float32), exponent_bits=8, mantissa_bits=7)
    gated = gated_f.astype(jnp.bfloat16)
    gated_t = gated.T.reshape(nb, sub * GROUP, own_rows)
    got = exchange(gated_t, nb, s, False)
    positions = jnp.arange(total_rows, dtype=jnp.int32).astype(jnp.float32)
    my_out = lax.dynamic_slice_in_dim(filter_out, s * sub, sub, 1)
    my_decay = lax.dynamic_slice_in_dim(decay, s * sub, sub, 0)
    filters = filter_table(positions, float(total_rows), filter_in, filter_bias, my_out, my_decay)
    lagged = filters.astype(jnp.float32).reshape(nb, own_rows, sub).transpose(0, 2, 1)
    filt = jnp.concatenate([jnp.zeros((1, sub, own_rows), jnp.float32), lagged], axis=0)
    s_arr = jnp.reshape(s, (1,)).astype(jnp.int32)
    conv_parts = toeplitz_conv(s_arr, filt, got)
    back = exchange(conv_parts, nb, s, True)
    order = source(s, jnp.arange(nb, dtype=jnp.int32), nb)
    back = jnp.take(back, order, axis=0)
    conv = back.reshape(width, own_rows).T.astype(jnp.float32)
    mixed = outer_gate.astype(jnp.float32) * (conv + skip_gain[None, :] * gated_f)
    return mixed.astype(jnp.bfloat16)


def solution(mesh):
    placed = (
        P(("groups", "seq"), "chan"),
        P(("groups", "seq"), "chan"),
        P(("groups", "seq"), "chan"),
        P(),
        P(),
        P(None, "chan"),
        P("chan"),
        P("chan"),
    )
    return jax.shard_map(
        per_device,
        mesh=mesh,
        in_specs=placed,
        out_specs=P(("groups", "seq"), "chan"),
        check_vma=False,
    )
```

```python
import functools

import jax
import jax.numpy as jnp
from jax import lax
from jax.experimental import pallas as pl
from jax.experimental.pallas import tpu as pltpu
from jax.sharding import PartitionSpec as P

GROUP = 16
BANDS = 16
FILTERS_PER_STEP = 16


def filter_table(positions, total, filter_in, filter_bias, filter_out, decay):
    bands = 2.8 * 0.7 ** jnp.arange(BANDS, dtype=jnp.float32)
    angles = positions[:, None] * bands[None, :]
    feats = jnp.concatenate(
        [(positions / total)[:, None], jnp.cos(angles), jnp.sin(angles)], axis=1
    )
    hidden = jnp.sin(
        10.0 * (jnp.dot(feats, filter_in, precision=lax.Precision.HIGHEST) + filter_bias[None, :])
    )
    raw = jnp.dot(hidden, filter_out, precision=lax.Precision.HIGHEST)
    envelope = jnp.sqrt(2.0 * decay)[None, :] * jnp.exp(-decay[None, :] * positions[:, None])
    return (raw * envelope).astype(jnp.bfloat16)


def toeplitz_kernel(s_ref, filt_ref, z_ref, o_ref, x_ref, acc_ref):
    nb = z_ref.shape[0]
    fb = filt_ref.shape[1]
    block = z_ref.shape[2]
    s = s_ref[0]
    upper = (lax.broadcasted_iota(jnp.int32, (block, block), 1)
             >= lax.broadcasted_iota(jnp.int32, (block, block), 0))
    for g in range(fb):
        ch = slice(g * GROUP, (g + 1) * GROUP)
        for j in range(nb):
            x_ref[j * GROUP:(j + 1) * GROUP, :] = z_ref[(s - j + nb) % nb, ch, :]
        acc_ref[...] = jnp.zeros(acc_ref.shape, jnp.float32)
        prev = None
        for d in range(nb):
            w = filt_ref[d + 1, pl.ds(g, block, stride=0), :]
            cur = pltpu.roll(w, 0, 1, stride=1, stride_axis=0)
            low = 0.0 if prev is None else prev
            t = jnp.where(upper, cur, low).astype(jnp.bfloat16)
            rows = (nb - d) * GROUP
            acc_ref[d * GROUP:, :] += jnp.dot(
                x_ref[:rows, :], t, preferred_element_type=jnp.float32
            )
            prev = cur
        for i in range(nb):
            o_ref[(i - s + nb) % nb, ch, :] = (
                acc_ref[i * GROUP:(i + 1) * GROUP, :].astype(jnp.bfloat16))


def toeplitz_conv(s, filt, z):
    nb, chans, block = z.shape
    count = chans // GROUP
    fb = min(FILTERS_PER_STEP, count)
    return pl.pallas_call(
        toeplitz_kernel,
        out_shape=jax.ShapeDtypeStruct((nb, chans, block), jnp.bfloat16),
        grid_spec=pltpu.PrefetchScalarGridSpec(
            num_scalar_prefetch=1,
            grid=(count // fb,),
            in_specs=[
                pl.BlockSpec((nb + 1, fb, block), lambda i, s_: (0, i, 0)),
                pl.BlockSpec((nb, fb * GROUP, block), lambda i, s_: (0, i, 0)),
            ],
            out_specs=pl.BlockSpec((nb, fb * GROUP, block), lambda i, s_: (0, i, 0)),
            scratch_shapes=[pltpu.VMEM((nb * GROUP, block), jnp.bfloat16),
                            pltpu.VMEM((nb * GROUP, block), jnp.float32)],
        ),
    )(s, filt, z)


def exchange(x, nb, s, ordered):
    got = [x[0] if ordered else lax.dynamic_index_in_dim(x, s, 0, keepdims=False)]
    for k in range(1, nb):
        if ordered:
            piece = x[k]
        else:
            piece = lax.dynamic_index_in_dim(x, (s + k) % nb, 0, keepdims=False)
        got.append(lax.ppermute(piece, "seq", [(i, (i + k) % nb) for i in range(nb)]))
    return jnp.stack(got)


def per_device(
    outer_gate, inner_gate, signal, filter_in, filter_bias, filter_out, decay, skip_gain
):
    own_rows, width = signal.shape
    nb = lax.axis_size("seq")
    total_rows = own_rows * nb
    s = lax.axis_index("seq")
    count = width // GROUP
    sub = count // nb
    gated_f = lax.reduce_precision(
        inner_gate.astype(jnp.float32) * signal.astype(jnp.float32), exponent_bits=8, mantissa_bits=7)
    gated = gated_f.astype(jnp.bfloat16)
    gated_t = gated.T.reshape(nb, sub * GROUP, own_rows)
    got = exchange(gated_t, nb, s, False)
    positions = jnp.arange(total_rows, dtype=jnp.int32).astype(jnp.float32)
    my_out = lax.dynamic_slice_in_dim(filter_out, s * sub, sub, 1)
    my_decay = lax.dynamic_slice_in_dim(decay, s * sub, sub, 0)
    filters = filter_table(positions, float(total_rows), filter_in, filter_bias, my_out, my_decay)
    lagged = filters.astype(jnp.float32).reshape(nb, own_rows, sub).transpose(0, 2, 1)
    filt = jnp.concatenate([jnp.zeros((1, sub, own_rows), jnp.float32), lagged], axis=0)
    s_arr = jnp.reshape(s, (1,)).astype(jnp.int32)
    conv_parts = toeplitz_conv(s_arr, filt, got)
    base = skip_gain[None, :] * gated_f
    back = exchange(conv_parts, nb, s, True)
    chunk = sub * GROUP
    conv_t = jnp.zeros((width, own_rows), jnp.bfloat16)
    for k in range(nb):
        conv_t = lax.dynamic_update_slice_in_dim(conv_t, back[k], ((s - k + nb) % nb) * chunk, 0)
    conv = conv_t.T.astype(jnp.float32)
    mixed = outer_gate.astype(jnp.float32) * (conv + base)
    return mixed.astype(jnp.bfloat16)


def solution(mesh):
    placed = (
        P(("groups", "seq"), "chan"),
        P(("groups", "seq"), "chan"),
        P(("groups", "seq"), "chan"),
        P(),
        P(),
        P(None, "chan"),
        P("chan"),
        P("chan"),
    )
    return jax.shard_map(
        per_device,
        mesh=mesh,
        in_specs=placed,
        out_specs=P(("groups", "seq"), "chan"),
        check_vma=False,
    )
```

```python
import jax
import jax.numpy as jnp
from jax import lax
from jax.experimental import pallas as pl
from jax.experimental.pallas import tpu as pltpu
from jax.sharding import PartitionSpec as P


GROUP = 16
BANDS = 16
FILTERS_PER_STEP = 16


def filter_table(positions, total, filter_in, filter_bias, filter_out, decay):
    bands = 2.8 * 0.7 ** jnp.arange(BANDS, dtype=jnp.float32)
    angles = positions[:, None] * bands[None, :]
    feats = jnp.concatenate(
        [(positions / total)[:, None], jnp.cos(angles), jnp.sin(angles)], axis=1
    )
    hidden = jnp.sin(
        10.0 * (jnp.dot(feats, filter_in, precision=lax.Precision.HIGHEST) + filter_bias[None, :])
    )
    raw = jnp.dot(hidden, filter_out, precision=lax.Precision.HIGHEST)
    envelope = jnp.sqrt(2.0 * decay)[None, :] * jnp.exp(-decay[None, :] * positions[:, None])
    return (raw * envelope).astype(jnp.bfloat16)


def toeplitz_kernel(s_ref, filt_ref, z_ref, o_ref, x_ref, acc_ref):
    nb = z_ref.shape[0]
    fb = filt_ref.shape[1]
    block = z_ref.shape[2]
    s = s_ref[0]
    upper = (lax.broadcasted_iota(jnp.int32, (block, block), 1)
             >= lax.broadcasted_iota(jnp.int32, (block, block), 0))
    for g in range(fb):
        ch = slice(g * GROUP, (g + 1) * GROUP)
        for j in range(nb):
            x_ref[j * GROUP:(j + 1) * GROUP, :] = z_ref[(s - j + nb) % nb, ch, :]
        acc_ref[...] = jnp.zeros(acc_ref.shape, jnp.float32)
        prev = None
        for d in range(nb):
            w = filt_ref[d + 1, pl.ds(g, block, stride=0), :]
            cur = pltpu.roll(w, 0, 1, stride=1, stride_axis=0)
            low = 0.0 if prev is None else prev
            t = jnp.where(upper, cur, low).astype(jnp.bfloat16)
            rows = (nb - d) * GROUP
            acc_ref[d * GROUP:, :] += jnp.dot(
                x_ref[:rows, :], t, preferred_element_type=jnp.float32
            )
            prev = cur
        for i in range(nb):
            o_ref[(i - s + nb) % nb, ch, :] = (
                acc_ref[i * GROUP:(i + 1) * GROUP, :].astype(jnp.bfloat16))


def toeplitz_conv(s, filt, z):
    nb, chans, block = z.shape
    count = chans // GROUP
    fb = min(FILTERS_PER_STEP, count)
    return pl.pallas_call(
        toeplitz_kernel,
        out_shape=jax.ShapeDtypeStruct((nb, chans, block), jnp.bfloat16),
        grid_spec=pltpu.PrefetchScalarGridSpec(
            num_scalar_prefetch=1,
            grid=(count // fb,),
            in_specs=[
                pl.BlockSpec((nb + 1, fb, block), lambda i, s_: (0, i, 0)),
                pl.BlockSpec((nb, fb * GROUP, block), lambda i, s_: (0, i, 0)),
            ],
            out_specs=pl.BlockSpec((nb, fb * GROUP, block), lambda i, s_: (0, i, 0)),
            scratch_shapes=[pltpu.VMEM((nb * GROUP, block), jnp.bfloat16),
                            pltpu.VMEM((nb * GROUP, block), jnp.float32)],
        ),
    )(s, filt, z)


def shift_order(nb):
    return sorted(range(1, nb), key=lambda k: (abs(2 * k - nb), k))


def exchange(x, nb, s, ordered):
    got = [None] * nb
    got[0] = x[0] if ordered else lax.dynamic_index_in_dim(x, s, 0, keepdims=False)
    for k in shift_order(nb):
        if ordered:
            piece = x[k]
        else:
            piece = lax.dynamic_index_in_dim(x, (s + k) % nb, 0, keepdims=False)
        got[k] = lax.ppermute(piece, "seq", [(i, (i + k) % nb) for i in range(nb)])
    return jnp.stack(got)


def mixer(
    outer_gate, inner_gate, signal, filter_in, filter_bias, filter_out, decay, skip_gain
):
    own_rows, width = signal.shape
    nb = lax.axis_size("seq")
    total_rows = own_rows * nb
    s = lax.axis_index("seq")
    count = width // GROUP
    sub = count // nb
    gated_f = lax.reduce_precision(
        inner_gate.astype(jnp.float32) * signal.astype(jnp.float32), exponent_bits=8, mantissa_bits=7)
    gated = gated_f.astype(jnp.bfloat16)
    gated_t = gated.T.reshape(nb, sub * GROUP, own_rows)
    got = exchange(gated_t, nb, s, False)
    positions = jnp.arange(total_rows, dtype=jnp.int32).astype(jnp.float32)
    my_out = lax.dynamic_slice_in_dim(filter_out, s * sub, sub, 1)
    my_decay = lax.dynamic_slice_in_dim(decay, s * sub, sub, 0)
    filters = filter_table(positions, float(total_rows), filter_in, filter_bias, my_out, my_decay)
    lagged = filters.astype(jnp.float32).reshape(nb, own_rows, sub).transpose(0, 2, 1)
    filt = jnp.concatenate([jnp.zeros((1, sub, own_rows), jnp.float32), lagged], axis=0)
    s_arr = jnp.reshape(s, (1,)).astype(jnp.int32)
    conv_parts = toeplitz_conv(s_arr, filt, got)
    back = exchange(conv_parts, nb, s, True)
    order = (s - jnp.arange(nb, dtype=jnp.int32) + nb) % nb
    back = jnp.take(back, order, axis=0)
    conv = back.reshape(width, own_rows).T.astype(jnp.float32)
    mixed = outer_gate.astype(jnp.float32) * (conv + skip_gain[None, :] * gated_f)
    return mixed.astype(jnp.bfloat16)


def solution(mesh):
    placed = (
        P(("groups", "seq"), "chan"),
        P(("groups", "seq"), "chan"),
        P(("groups", "seq"), "chan"),
        P(),
        P(),
        P(None, "chan"),
        P("chan"),
        P("chan"),
    )
    return jax.shard_map(
        mixer,
        mesh=mesh,
        in_specs=placed,
        out_specs=P(("groups", "seq"), "chan"),
        check_vma=False,
    )
```

```python
import functools

import jax
import jax.numpy as jnp
from jax import lax
from jax.experimental import pallas as pl
from jax.experimental.pallas import tpu as pltpu
from jax.sharding import PartitionSpec as P

GROUP = 16
BANDS = 16
FILTERS_PER_STEP = 16


def filter_table(positions, total, filter_in, filter_bias, filter_out, decay):
    bands = 2.8 * 0.7 ** jnp.arange(BANDS, dtype=jnp.float32)
    angles = positions[:, None] * bands[None, :]
    feats = jnp.concatenate(
        [(positions / total)[:, None], jnp.cos(angles), jnp.sin(angles)], axis=1
    )
    hidden = jnp.sin(
        10.0 * (jnp.dot(feats, filter_in, precision=lax.Precision.HIGHEST) + filter_bias[None, :])
    )
    raw = jnp.dot(hidden, filter_out, precision=lax.Precision.HIGHEST)
    envelope = jnp.sqrt(2.0 * decay)[None, :] * jnp.exp(-decay[None, :] * positions[:, None])
    return (raw * envelope).astype(jnp.bfloat16)


def toeplitz_kernel(s_ref, filt_ref, *refs):
    nb = filt_ref.shape[0] - 1
    z_refs = refs[:nb]
    o_ref, x_ref, acc_ref = refs[nb:]
    fb = filt_ref.shape[1]
    block = filt_ref.shape[2]
    s = s_ref[0]
    upper = (lax.broadcasted_iota(jnp.int32, (block, block), 1)
             >= lax.broadcasted_iota(jnp.int32, (block, block), 0))
    for g in range(fb):
        ch = slice(g * GROUP, (g + 1) * GROUP)
        for k in range(nb):
            j = (s - k + nb) % nb
            x_ref[pl.ds(pl.multiple_of(j * GROUP, GROUP), GROUP), :] = z_refs[k][ch, :]
        prev = None
        for d in range(nb):
            w = filt_ref[d + 1, pl.ds(g, block, stride=0), :]
            cur = pltpu.roll(w, 0, 1, stride=1, stride_axis=0)
            low = 0.0 if prev is None else prev
            t = jnp.where(upper, cur, low).astype(jnp.bfloat16)
            rows = (nb - d) * GROUP
            part = jnp.dot(x_ref[:rows, :], t, preferred_element_type=jnp.float32)
            if d == 0:
                acc_ref[...] = part
            else:
                acc_ref[d * GROUP:, :] += part
            prev = cur
        for i in range(nb):
            o_ref[(i - s + nb) % nb, ch, :] = (
                acc_ref[i * GROUP:(i + 1) * GROUP, :].astype(jnp.bfloat16))


def toeplitz_conv(s, filt, pieces):
    nb = len(pieces)
    chans, block = pieces[0].shape
    count = chans // GROUP
    fb = min(FILTERS_PER_STEP, count)
    return pl.pallas_call(
        toeplitz_kernel,
        out_shape=jax.ShapeDtypeStruct((nb, chans, block), jnp.bfloat16),
        grid_spec=pltpu.PrefetchScalarGridSpec(
            num_scalar_prefetch=1,
            grid=(count // fb,),
            in_specs=[pl.BlockSpec((nb + 1, fb, block), lambda i, s_: (0, i, 0))]
            + [pl.BlockSpec((fb * GROUP, block), lambda i, s_: (i, 0))] * nb,
            out_specs=pl.BlockSpec((nb, fb * GROUP, block), lambda i, s_: (0, i, 0)),
            scratch_shapes=[pltpu.VMEM((nb * GROUP, block), jnp.bfloat16),
                            pltpu.VMEM((nb * GROUP, block), jnp.float32)],
        ),
    )(s, filt, *pieces)


def exchange(x, nb, s, ordered):
    got = [x[0] if ordered else lax.dynamic_index_in_dim(x, s, 0, keepdims=False)]
    for k in range(1, nb):
        if ordered:
            piece = x[k]
        else:
            piece = lax.dynamic_index_in_dim(x, (s + k) % nb, 0, keepdims=False)
        got.append(lax.ppermute(piece, "seq", [(i, (i + k) % nb) for i in range(nb)]))
    return got


def per_device(
    outer_gate, inner_gate, signal, filter_in, filter_bias, filter_out, decay, skip_gain
):
    own_rows, width = signal.shape
    nb = lax.axis_size("seq")
    total_rows = own_rows * nb
    s = lax.axis_index("seq")
    count = width // GROUP
    sub = count // nb
    gated_f = lax.reduce_precision(
        inner_gate.astype(jnp.float32) * signal.astype(jnp.float32), exponent_bits=8, mantissa_bits=7)
    gated = gated_f.astype(jnp.bfloat16)
    gated_t = gated.T.reshape(nb, sub * GROUP, own_rows)
    got = exchange(gated_t, nb, s, False)
    positions = jnp.arange(total_rows, dtype=jnp.int32).astype(jnp.float32)
    my_out = lax.dynamic_slice_in_dim(filter_out, s * sub, sub, 1)
    my_decay = lax.dynamic_slice_in_dim(decay, s * sub, sub, 0)
    filters = filter_table(positions, float(total_rows), filter_in, filter_bias, my_out, my_decay)
    lagged = filters.astype(jnp.float32).reshape(nb, own_rows, sub).transpose(0, 2, 1)
    filt = jnp.concatenate([jnp.zeros((1, sub, own_rows), jnp.float32), lagged], axis=0)
    s_arr = jnp.reshape(s, (1,)).astype(jnp.int32)
    conv_parts = toeplitz_conv(s_arr, filt, got)
    back = jnp.stack(exchange(conv_parts, nb, s, True))
    order = (s - jnp.arange(nb, dtype=jnp.int32) + nb) % nb
    back = jnp.take(back, order, axis=0)
    conv = back.reshape(width, own_rows).T.astype(jnp.float32)
    mixed = outer_gate.astype(jnp.float32) * (conv + skip_gain[None, :] * gated_f)
    return mixed.astype(jnp.bfloat16)


def solution(mesh):
    placed = (
        P(("groups", "seq"), "chan"),
        P(("groups", "seq"), "chan"),
        P(("groups", "seq"), "chan"),
        P(),
        P(),
        P(None, "chan"),
        P("chan"),
        P("chan"),
    )
    return jax.shard_map(
        per_device,
        mesh=mesh,
        in_specs=placed,
        out_specs=P(("groups", "seq"), "chan"),
        check_vma=False,
    )
```

```python
import functools

import jax
import jax.numpy as jnp
from jax import lax
from jax.experimental import pallas as pl
from jax.experimental.pallas import tpu as pltpu
from jax.sharding import PartitionSpec as P

GROUP = 16
BANDS = 16
FILTERS_PER_STEP = 16


def filter_table(positions, total, filter_in, filter_bias, filter_out, decay):
    bands = 2.8 * 0.7 ** jnp.arange(BANDS, dtype=jnp.float32)
    angles = positions[:, None] * bands[None, :]
    feats = jnp.concatenate(
        [(positions / total)[:, None], jnp.cos(angles), jnp.sin(angles)], axis=1
    )
    hidden = jnp.sin(
        10.0 * (jnp.dot(feats, filter_in, precision=lax.Precision.HIGHEST) + filter_bias[None, :])
    )
    raw = jnp.dot(hidden, filter_out, precision=lax.Precision.HIGHEST)
    envelope = jnp.sqrt(2.0 * decay)[None, :] * jnp.exp(-decay[None, :] * positions[:, None])
    return (raw * envelope).astype(jnp.bfloat16)


def toeplitz_kernel(s_ref, filt_ref, z_ref, *refs):
    nb = z_ref.shape[0]
    o_refs = refs[:nb]
    x_ref, acc_ref = refs[nb:]
    fb = filt_ref.shape[1]
    block = z_ref.shape[2]
    s = s_ref[0]
    upper = (lax.broadcasted_iota(jnp.int32, (block, block), 1)
             >= lax.broadcasted_iota(jnp.int32, (block, block), 0))
    for g in range(fb):
        ch = slice(g * GROUP, (g + 1) * GROUP)
        for j in range(nb):
            x_ref[j * GROUP:(j + 1) * GROUP, :] = z_ref[(s - j + nb) % nb, ch, :]
        acc_ref[...] = jnp.zeros(acc_ref.shape, jnp.float32)
        prev = None
        for d in range(nb):
            w = filt_ref[d + 1, pl.ds(g, block, stride=0), :]
            cur = pltpu.roll(w, 0, 1, stride=1, stride_axis=0)
            low = 0.0 if prev is None else prev
            t = jnp.where(upper, cur, low).astype(jnp.bfloat16)
            rows = (nb - d) * GROUP
            acc_ref[d * GROUP:, :] += jnp.dot(
                x_ref[:rows, :], t, preferred_element_type=jnp.float32
            )
            prev = cur
        for k in range(nb):
            i = (s + k) % nb
            o_refs[k][ch, :] = acc_ref[pl.ds(pl.multiple_of(i * GROUP, GROUP), GROUP), :].astype(
                jnp.bfloat16)


def toeplitz_conv(s, filt, z):
    nb, chans, block = z.shape
    count = chans // GROUP
    fb = min(FILTERS_PER_STEP, count)
    return pl.pallas_call(
        toeplitz_kernel,
        out_shape=[jax.ShapeDtypeStruct((chans, block), jnp.bfloat16) for _ in range(nb)],
        grid_spec=pltpu.PrefetchScalarGridSpec(
            num_scalar_prefetch=1,
            grid=(count // fb,),
            in_specs=[
                pl.BlockSpec((nb + 1, fb, block), lambda i, s_: (0, i, 0)),
                pl.BlockSpec((nb, fb * GROUP, block), lambda i, s_: (0, i, 0)),
            ],
            out_specs=[pl.BlockSpec((fb * GROUP, block), lambda i, s_: (i, 0))] * nb,
            scratch_shapes=[pltpu.VMEM((nb * GROUP, block), jnp.bfloat16),
                            pltpu.VMEM((nb * GROUP, block), jnp.float32)],
        ),
    )(s, filt, z)


def exchange(x, nb, s, ordered):
    got = [x[0] if ordered else lax.dynamic_index_in_dim(x, s, 0, keepdims=False)]
    for k in range(1, nb):
        if ordered:
            piece = x[k]
        else:
            piece = lax.dynamic_index_in_dim(x, (s + k) % nb, 0, keepdims=False)
        got.append(lax.ppermute(piece, "seq", [(i, (i + k) % nb) for i in range(nb)]))
    return jnp.stack(got)


def per_device(
    outer_gate, inner_gate, signal, filter_in, filter_bias, filter_out, decay, skip_gain
):
    own_rows, width = signal.shape
    nb = lax.axis_size("seq")
    total_rows = own_rows * nb
    s = lax.axis_index("seq")
    count = width // GROUP
    sub = count // nb
    gated_f = lax.reduce_precision(
        inner_gate.astype(jnp.float32) * signal.astype(jnp.float32), exponent_bits=8, mantissa_bits=7)
    gated = gated_f.astype(jnp.bfloat16)
    gated_t = gated.T.reshape(nb, sub * GROUP, own_rows)
    got = exchange(gated_t, nb, s, False)
    positions = jnp.arange(total_rows, dtype=jnp.int32).astype(jnp.float32)
    my_out = lax.dynamic_slice_in_dim(filter_out, s * sub, sub, 1)
    my_decay = lax.dynamic_slice_in_dim(decay, s * sub, sub, 0)
    filters = filter_table(positions, float(total_rows), filter_in, filter_bias, my_out, my_decay)
    lagged = filters.astype(jnp.float32).reshape(nb, own_rows, sub).transpose(0, 2, 1)
    filt = jnp.concatenate([jnp.zeros((1, sub, own_rows), jnp.float32), lagged], axis=0)
    s_arr = jnp.reshape(s, (1,)).astype(jnp.int32)
    conv_parts = toeplitz_conv(s_arr, filt, got)
    back = exchange(conv_parts, nb, s, True)
    order = (s - jnp.arange(nb, dtype=jnp.int32) + nb) % nb
    back = jnp.take(back, order, axis=0)
    conv = back.reshape(width, own_rows).T.astype(jnp.float32)
    mixed = outer_gate.astype(jnp.float32) * (conv + skip_gain[None, :] * gated_f)
    return mixed.astype(jnp.bfloat16)


def solution(mesh):
    placed = (
        P(("groups", "seq"), "chan"),
        P(("groups", "seq"), "chan"),
        P(("groups", "seq"), "chan"),
        P(),
        P(),
        P(None, "chan"),
        P("chan"),
        P("chan"),
    )
    return jax.shard_map(
        per_device,
        mesh=mesh,
        in_specs=placed,
        out_specs=P(("groups", "seq"), "chan"),
        check_vma=False,
    )
```

```python
import functools

import jax
import jax.numpy as jnp
from jax import lax
from jax.experimental import pallas as pl
from jax.experimental.pallas import tpu as pltpu
from jax.sharding import PartitionSpec as P

GROUP = 16
BANDS = 16
FILTERS_PER_STEP = 16


def filter_table(positions, total, filter_in, filter_bias, filter_out, decay):
    bands = 2.8 * 0.7 ** jnp.arange(BANDS, dtype=jnp.float32)
    angles = positions[:, None] * bands[None, :]
    feats = jnp.concatenate(
        [(positions / total)[:, None], jnp.cos(angles), jnp.sin(angles)], axis=1
    )
    hidden = jnp.sin(
        10.0 * (jnp.dot(feats, filter_in, precision=lax.Precision.HIGHEST) + filter_bias[None, :])
    )
    raw = jnp.dot(hidden, filter_out, precision=lax.Precision.HIGHEST)
    envelope = jnp.sqrt(2.0 * decay)[None, :] * jnp.exp(-decay[None, :] * positions[:, None])
    return (raw * envelope).astype(jnp.bfloat16)


def toeplitz_kernel(s_ref, filt_ref, z_ref, *refs):
    nb = z_ref.shape[0]
    o_refs = refs[:nb]
    x_ref, acc_ref = refs[nb:]
    fb = filt_ref.shape[1]
    block = z_ref.shape[2]
    s = s_ref[0]
    upper = (lax.broadcasted_iota(jnp.int32, (block, block), 1)
             >= lax.broadcasted_iota(jnp.int32, (block, block), 0))
    for g in range(fb):
        ch = slice(g * GROUP, (g + 1) * GROUP)
        for j in range(nb):
            x_ref[j * GROUP:(j + 1) * GROUP, :] = z_ref[(s - j + nb) % nb, ch, :]
        acc_ref[...] = jnp.zeros(acc_ref.shape, jnp.float32)
        prev = None
        for d in range(nb):
            w = filt_ref[d + 1, pl.ds(g, block, stride=0), :]
            cur = pltpu.roll(w, 0, 1, stride=1, stride_axis=0)
            low = 0.0 if prev is None else prev
            t = jnp.where(upper, cur, low).astype(jnp.bfloat16)
            rows = (nb - d) * GROUP
            acc_ref[d * GROUP:, :] += jnp.dot(
                x_ref[:rows, :], t, preferred_element_type=jnp.float32
            )
            prev = cur
        for k in range(nb):
            i = (s + k) % nb
            o_refs[k][ch, :] = acc_ref[pl.ds(pl.multiple_of(i * GROUP, GROUP), GROUP), :].astype(
                jnp.bfloat16)


def toeplitz_conv(s, filt, z):
    nb, chans, block = z.shape
    count = chans // GROUP
    fb = min(FILTERS_PER_STEP, count)
    return pl.pallas_call(
        toeplitz_kernel,
        out_shape=[jax.ShapeDtypeStruct((chans, block), jnp.bfloat16) for _ in range(nb)],
        grid_spec=pltpu.PrefetchScalarGridSpec(
            num_scalar_prefetch=1,
            grid=(count // fb,),
            in_specs=[
                pl.BlockSpec((nb + 1, fb, block), lambda i, s_: (0, i, 0)),
                pl.BlockSpec((nb, fb * GROUP, block), lambda i, s_: (0, i, 0)),
            ],
            out_specs=[pl.BlockSpec((fb * GROUP, block), lambda i, s_: (i, 0))] * nb,
            scratch_shapes=[pltpu.VMEM((nb * GROUP, block), jnp.bfloat16),
                            pltpu.VMEM((nb * GROUP, block), jnp.float32)],
        ),
    )(s, filt, z)


def exchange(x, nb, s, ordered):
    got = [x[0] if ordered else lax.dynamic_index_in_dim(x, s, 0, keepdims=False)]
    for k in range(1, nb):
        if ordered:
            piece = x[k]
        else:
            piece = lax.dynamic_index_in_dim(x, (s + k) % nb, 0, keepdims=False)
        got.append(lax.ppermute(piece, "seq", [(i, (i + k) % nb) for i in range(nb)]))
    return got


def per_device(
    outer_gate, inner_gate, signal, filter_in, filter_bias, filter_out, decay, skip_gain
):
    own_rows, width = signal.shape
    nb = lax.axis_size("seq")
    total_rows = own_rows * nb
    s = lax.axis_index("seq")
    count = width // GROUP
    sub = count // nb
    gated_f = lax.reduce_precision(
        inner_gate.astype(jnp.float32) * signal.astype(jnp.float32), exponent_bits=8, mantissa_bits=7)
    gated = gated_f.astype(jnp.bfloat16)
    gated_t = gated.T.reshape(nb, sub * GROUP, own_rows)
    got = exchange(gated_t, nb, s, False)
    positions = jnp.arange(total_rows, dtype=jnp.int32).astype(jnp.float32)
    my_out = lax.dynamic_slice_in_dim(filter_out, s * sub, sub, 1)
    my_decay = lax.dynamic_slice_in_dim(decay, s * sub, sub, 0)
    filters = filter_table(positions, float(total_rows), filter_in, filter_bias, my_out, my_decay)
    lagged = filters.astype(jnp.float32).reshape(nb, own_rows, sub).transpose(0, 2, 1)
    filt = jnp.concatenate([jnp.zeros((1, sub, own_rows), jnp.float32), lagged], axis=0)
    s_arr = jnp.reshape(s, (1,)).astype(jnp.int32)
    conv_parts = toeplitz_conv(s_arr, filt, jnp.stack(got))
    back = exchange(conv_parts, nb, s, True)
    chunks = []
    for c in range(nb):
        src_k = (s - c + nb) % nb
        piece = back[0]
        for k in range(1, nb):
            piece = jnp.where(src_k == k, back[k], piece)
        chunks.append(piece)
    back = jnp.concatenate(chunks, axis=0)
    conv = back.reshape(width, own_rows).T.astype(jnp.float32)
    mixed = outer_gate.astype(jnp.float32) * (conv + skip_gain[None, :] * gated_f)
    return mixed.astype(jnp.bfloat16)


def solution(mesh):
    placed = (
        P(("groups", "seq"), "chan"),
        P(("groups", "seq"), "chan"),
        P(("groups", "seq"), "chan"),
        P(),
        P(),
        P(None, "chan"),
        P("chan"),
        P("chan"),
    )
    return jax.shard_map(
        per_device,
        mesh=mesh,
        in_specs=placed,
        out_specs=P(("groups", "seq"), "chan"),
        check_vma=False,
    )
```

```python
import functools

import jax
import jax.numpy as jnp
from jax import lax
from jax.experimental import pallas as pl
from jax.experimental.pallas import tpu as pltpu
from jax.sharding import PartitionSpec as P

GROUP = 16
BANDS = 16
FILTERS_PER_STEP = 16


def filter_table(positions, total, filter_in, filter_bias, filter_out, decay):
    bands = 2.8 * 0.7 ** jnp.arange(BANDS, dtype=jnp.float32)
    angles = positions[:, None] * bands[None, :]
    feats = jnp.concatenate(
        [(positions / total)[:, None], jnp.cos(angles), jnp.sin(angles)], axis=1
    )
    hidden = jnp.sin(
        10.0 * (jnp.dot(feats, filter_in, precision=lax.Precision.HIGHEST) + filter_bias[None, :])
    )
    raw = jnp.dot(hidden, filter_out, precision=lax.Precision.HIGHEST)
    envelope = jnp.sqrt(2.0 * decay)[None, :] * jnp.exp(-decay[None, :] * positions[:, None])
    return (raw * envelope).astype(jnp.bfloat16)


def toeplitz_kernel(s_ref, filt_ref, z_ref, o_ref, x_ref, acc_ref):
    nb = z_ref.shape[0]
    fb = filt_ref.shape[1]
    block = z_ref.shape[2]
    s = s_ref[0]
    upper = (lax.broadcasted_iota(jnp.int32, (block, block), 1)
             >= lax.broadcasted_iota(jnp.int32, (block, block), 0))
    for g in range(fb):
        ch = slice(g * GROUP, (g + 1) * GROUP)
        for j in range(nb):
            x_ref[j * GROUP:(j + 1) * GROUP, :] = z_ref[(s - j + nb) % nb, ch, :]
        acc_ref[...] = jnp.zeros(acc_ref.shape, jnp.float32)
        prev = None
        for d in range(nb):
            w = filt_ref[d + 1, pl.ds(g, block, stride=0), :]
            cur = pltpu.roll(w, 0, 1, stride=1, stride_axis=0)
            low = 0.0 if prev is None else prev
            t = jnp.where(upper, cur, low).astype(jnp.bfloat16)
            rows = (nb - d) * GROUP
            acc_ref[d * GROUP:, :] += jnp.dot(
                x_ref[:rows, :], t, preferred_element_type=jnp.float32
            )
            prev = cur
        for i in range(nb):
            o_ref[(i - s + nb) % nb, ch, :] = (
                acc_ref[i * GROUP:(i + 1) * GROUP, :].astype(jnp.bfloat16))


def toeplitz_conv(s, filt, z):
    nb, chans, block = z.shape
    count = chans // GROUP
    fb = min(FILTERS_PER_STEP, count)
    return pl.pallas_call(
        toeplitz_kernel,
        out_shape=jax.ShapeDtypeStruct((nb, chans, block), jnp.bfloat16),
        grid_spec=pltpu.PrefetchScalarGridSpec(
            num_scalar_prefetch=1,
            grid=(count // fb,),
            in_specs=[
                pl.BlockSpec((nb + 1, fb, block), lambda i, s_: (0, i, 0)),
                pl.BlockSpec((nb, fb * GROUP, block), lambda i, s_: (0, i, 0)),
            ],
            out_specs=pl.BlockSpec((nb, fb * GROUP, block), lambda i, s_: (0, i, 0)),
            scratch_shapes=[pltpu.VMEM((nb * GROUP, block), jnp.bfloat16),
                            pltpu.VMEM((nb * GROUP, block), jnp.float32)],
        ),
    )(s, filt, z)


def exchange(x, nb, s, ordered):
    got = [x[0] if ordered else lax.dynamic_index_in_dim(x, s, 0, keepdims=False)]
    for k in range(1, nb):
        if ordered:
            piece = x[k]
        else:
            piece = lax.dynamic_index_in_dim(x, (s + k) % nb, 0, keepdims=False)
        got.append(lax.ppermute(piece, "seq", [(i, (i + k) % nb) for i in range(nb)]))
    return jnp.stack(got)


def per_device(
    outer_gate, inner_gate, signal, filter_in, filter_bias, filter_out, decay, skip_gain
):
    own_rows, width = signal.shape
    nb = lax.axis_size("seq")
    total_rows = own_rows * nb
    s = lax.axis_index("seq")
    count = width // GROUP
    sub = count // nb
    gated_f = lax.reduce_precision(
        inner_gate.astype(jnp.float32) * signal.astype(jnp.float32), exponent_bits=8, mantissa_bits=7)
    gated = gated_f.astype(jnp.bfloat16)
    gated_t = gated.T.reshape(nb, sub * GROUP, own_rows)
    got = exchange(gated_t, nb, s, False)
    positions = jnp.arange(total_rows, dtype=jnp.int32).astype(jnp.float32)
    my_out = lax.dynamic_slice_in_dim(filter_out, s * sub, sub, 1)
    my_decay = lax.dynamic_slice_in_dim(decay, s * sub, sub, 0)
    filters = filter_table(positions, float(total_rows), filter_in, filter_bias, my_out, my_decay)
    lagged = filters.astype(jnp.float32).reshape(nb, own_rows, sub).transpose(0, 2, 1)
    filt = jnp.concatenate([jnp.zeros((1, sub, own_rows), jnp.float32), lagged], axis=0)
    s_arr = jnp.reshape(s, (1,)).astype(jnp.int32)
    conv_parts = toeplitz_conv(s_arr, filt, got)
    back = exchange(conv_parts, nb, s, True)
    order = (s - jnp.arange(nb, dtype=jnp.int32) + nb) % nb
    back = jnp.take(back, order, axis=0)
    conv = lax.optimization_barrier(back.reshape(width, own_rows).T).astype(jnp.float32)
    mixed = outer_gate.astype(jnp.float32) * (conv + skip_gain[None, :] * gated_f)
    return mixed.astype(jnp.bfloat16)


def solution(mesh):
    placed = (
        P(("groups", "seq"), "chan"),
        P(("groups", "seq"), "chan"),
        P(("groups", "seq"), "chan"),
        P(),
        P(),
        P(None, "chan"),
        P("chan"),
        P("chan"),
    )
    return jax.shard_map(
        per_device,
        mesh=mesh,
        in_specs=placed,
        out_specs=P(("groups", "seq"), "chan"),
        check_vma=False,
    )
```

```python
import functools

import jax
import jax.numpy as jnp
from jax import lax
from jax.experimental import pallas as pl
from jax.experimental.pallas import tpu as pltpu
from jax.sharding import PartitionSpec as P

GROUP = 16
BANDS = 16
FILTERS_PER_STEP = 16


def filter_table(positions, total, filter_in, filter_bias, filter_out, decay):
    bands = 2.8 * 0.7 ** jnp.arange(BANDS, dtype=jnp.float32)
    angles = positions[:, None] * bands[None, :]
    feats = jnp.concatenate(
        [(positions / total)[:, None], jnp.cos(angles), jnp.sin(angles)], axis=1
    )
    hidden = jnp.sin(
        10.0 * (jnp.dot(feats, filter_in, precision=lax.Precision.HIGHEST) + filter_bias[None, :])
    )
    raw = jnp.dot(hidden, filter_out, precision=lax.Precision.HIGHEST)
    envelope = jnp.sqrt(2.0 * decay)[None, :] * jnp.exp(-decay[None, :] * positions[:, None])
    return (raw * envelope).astype(jnp.bfloat16)


def toeplitz_kernel(s_ref, filt_ref, z_ref, o_ref, x_ref, acc_ref):
    nb = z_ref.shape[0]
    fb = filt_ref.shape[1]
    block = z_ref.shape[2]
    s = s_ref[0]
    upper = (lax.broadcasted_iota(jnp.int32, (block, block), 1)
             >= lax.broadcasted_iota(jnp.int32, (block, block), 0))
    for g in range(fb):
        ch = slice(g * GROUP, (g + 1) * GROUP)
        for j in range(nb):
            x_ref[j * GROUP:(j + 1) * GROUP, :] = z_ref[(s - j + nb) % nb, ch, :]
        acc_ref[...] = jnp.zeros(acc_ref.shape, jnp.float32)
        prev = None
        for d in range(nb):
            w = filt_ref[d + 1, pl.ds(g, block, stride=0), :]
            cur = pltpu.roll(w, 0, 1, stride=1, stride_axis=0)
            low = 0.0 if prev is None else prev
            t = jnp.where(upper, cur, low).astype(jnp.bfloat16)
            rows = (nb - d) * GROUP
            acc_ref[d * GROUP:, :] += jnp.dot(
                x_ref[:rows, :], t, preferred_element_type=jnp.float32
            )
            prev = cur
        for i in range(nb):
            o_ref[(i - s + nb) % nb, ch, :] = (
                acc_ref[i * GROUP:(i + 1) * GROUP, :].astype(jnp.bfloat16))


def toeplitz_conv(s, filt, z):
    nb, chans, block = z.shape
    count = chans // GROUP
    fb = min(FILTERS_PER_STEP, count)
    return pl.pallas_call(
        toeplitz_kernel,
        out_shape=jax.ShapeDtypeStruct((nb, chans, block), jnp.bfloat16),
        grid_spec=pltpu.PrefetchScalarGridSpec(
            num_scalar_prefetch=1,
            grid=(count // fb,),
            in_specs=[
                pl.BlockSpec((nb + 1, fb, block), lambda i, s_: (0, i, 0)),
                pl.BlockSpec((nb, fb * GROUP, block), lambda i, s_: (0, i, 0)),
            ],
            out_specs=pl.BlockSpec((nb, fb * GROUP, block), lambda i, s_: (0, i, 0)),
            scratch_shapes=[pltpu.VMEM((nb * GROUP, block), jnp.bfloat16),
                            pltpu.VMEM((nb * GROUP, block), jnp.float32)],
        ),
    )(s, filt, z)


def exchange(x, nb, s, ordered):
    got = [x[0] if ordered else lax.dynamic_index_in_dim(x, s, 0, keepdims=False)]
    for k in range(1, nb):
        if ordered:
            piece = x[k]
        else:
            piece = lax.dynamic_index_in_dim(x, (s + k) % nb, 0, keepdims=False)
        got.append(lax.ppermute(piece, "seq", [(i, (i + k) % nb) for i in range(nb)]))
    return jnp.stack(got)


def per_device(
    outer_gate, inner_gate, signal, filter_in, filter_bias, filter_out, decay, skip_gain
):
    own_rows, width = signal.shape
    nb = lax.axis_size("seq")
    total_rows = own_rows * nb
    s = lax.axis_index("seq")
    count = width // GROUP
    sub = count // nb
    gated_f = lax.reduce_precision(
        inner_gate.astype(jnp.float32) * signal.astype(jnp.float32), exponent_bits=8, mantissa_bits=7)
    gated = gated_f.astype(jnp.bfloat16)
    chunk = sub * GROUP
    pieces = []
    for k in range(nb):
        start = ((s + k) % nb) * chunk
        part = lax.reduce_precision(
            lax.dynamic_slice_in_dim(inner_gate, start, chunk, 1).astype(jnp.float32)
            * lax.dynamic_slice_in_dim(signal, start, chunk, 1).astype(jnp.float32),
            exponent_bits=8, mantissa_bits=7)
        pieces.append(part.astype(jnp.bfloat16).T)
    got = exchange(pieces, nb, s, True)
    positions = jnp.arange(total_rows, dtype=jnp.int32).astype(jnp.float32)
    my_out = lax.dynamic_slice_in_dim(filter_out, s * sub, sub, 1)
    my_decay = lax.dynamic_slice_in_dim(decay, s * sub, sub, 0)
    filters = filter_table(positions, float(total_rows), filter_in, filter_bias, my_out, my_decay)
    lagged = filters.astype(jnp.float32).reshape(nb, own_rows, sub).transpose(0, 2, 1)
    filt = jnp.concatenate([jnp.zeros((1, sub, own_rows), jnp.float32), lagged], axis=0)
    s_arr = jnp.reshape(s, (1,)).astype(jnp.int32)
    conv_parts = toeplitz_conv(s_arr, filt, got)
    back = exchange(conv_parts, nb, s, True)
    order = (s - jnp.arange(nb, dtype=jnp.int32) + nb) % nb
    back = jnp.take(back, order, axis=0)
    conv = back.reshape(width, own_rows).T.astype(jnp.float32)
    mixed = outer_gate.astype(jnp.float32) * (conv + skip_gain[None, :] * gated_f)
    return mixed.astype(jnp.bfloat16)


def solution(mesh):
    placed = (
        P(("groups", "seq"), "chan"),
        P(("groups", "seq"), "chan"),
        P(("groups", "seq"), "chan"),
        P(),
        P(),
        P(None, "chan"),
        P("chan"),
        P("chan"),
    )
    return jax.shard_map(
        per_device,
        mesh=mesh,
        in_specs=placed,
        out_specs=P(("groups", "seq"), "chan"),
        check_vma=False,
    )
```

```python
import functools

import jax
import jax.numpy as jnp
from jax import lax
from jax.experimental import pallas as pl
from jax.experimental.pallas import tpu as pltpu
from jax.sharding import PartitionSpec as P

GROUP = 16
BANDS = 16
FILTERS_PER_STEP = 16


def filter_table(positions, total, filter_in, filter_bias, filter_out, decay):
    bands = 2.8 * 0.7 ** jnp.arange(BANDS, dtype=jnp.float32)
    angles = positions[:, None] * bands[None, :]
    feats = jnp.concatenate(
        [(positions / total)[:, None], jnp.cos(angles), jnp.sin(angles)], axis=1
    )
    hidden = jnp.sin(
        10.0 * (jnp.dot(feats, filter_in, precision=lax.Precision.HIGHEST) + filter_bias[None, :])
    )
    raw = jnp.dot(hidden, filter_out, precision=lax.Precision.HIGHEST)
    envelope = jnp.sqrt(2.0 * decay)[None, :] * jnp.exp(-decay[None, :] * positions[:, None])
    return (raw * envelope).astype(jnp.bfloat16)


def toeplitz_kernel(s_ref, filt_ref, z_ref, *refs):
    nb = z_ref.shape[0]
    o_refs = refs[:nb]
    x_ref, acc_ref = refs[nb:]
    fb = filt_ref.shape[1]
    block = z_ref.shape[2]
    s = s_ref[0]
    upper = (lax.broadcasted_iota(jnp.int32, (block, block), 1)
             >= lax.broadcasted_iota(jnp.int32, (block, block), 0))
    for g in range(fb):
        ch = slice(g * GROUP, (g + 1) * GROUP)
        for j in range(nb):
            x_ref[j * GROUP:(j + 1) * GROUP, :] = z_ref[(s - j + nb) % nb, ch, :]
        acc_ref[...] = jnp.zeros(acc_ref.shape, jnp.float32)
        prev = None
        for d in range(nb):
            w = filt_ref[d + 1, pl.ds(g, block, stride=0), :]
            cur = pltpu.roll(w, 0, 1, stride=1, stride_axis=0)
            low = 0.0 if prev is None else prev
            t = jnp.where(upper, cur, low).astype(jnp.bfloat16)
            rows = (nb - d) * GROUP
            acc_ref[d * GROUP:, :] += jnp.dot(
                x_ref[:rows, :], t, preferred_element_type=jnp.float32
            )
            prev = cur
        for k in range(nb):
            i = (s + k) % nb
            o_refs[k][ch, :] = acc_ref[pl.ds(pl.multiple_of(i * GROUP, GROUP), GROUP), :].astype(
                jnp.bfloat16)


def toeplitz_conv(s, filt, z):
    nb, chans, block = z.shape
    count = chans // GROUP
    fb = min(FILTERS_PER_STEP, count)
    return pl.pallas_call(
        toeplitz_kernel,
        out_shape=[jax.ShapeDtypeStruct((chans, block), jnp.bfloat16) for _ in range(nb)],
        grid_spec=pltpu.PrefetchScalarGridSpec(
            num_scalar_prefetch=1,
            grid=(count // fb,),
            in_specs=[
                pl.BlockSpec((nb + 1, fb, block), lambda i, s_: (0, i, 0)),
                pl.BlockSpec((nb, fb * GROUP, block), lambda i, s_: (0, i, 0)),
            ],
            out_specs=[pl.BlockSpec((fb * GROUP, block), lambda i, s_: (i, 0))] * nb,
            scratch_shapes=[pltpu.VMEM((nb * GROUP, block), jnp.bfloat16),
                            pltpu.VMEM((nb * GROUP, block), jnp.float32)],
        ),
    )(s, filt, z)


def exchange(x, nb, s, ordered):
    got = [x[0] if ordered else lax.dynamic_index_in_dim(x, s, 0, keepdims=False)]
    for k in range(1, nb):
        if ordered:
            piece = x[k]
        else:
            piece = lax.dynamic_index_in_dim(x, (s + k) % nb, 0, keepdims=False)
        got.append(lax.ppermute(piece, "seq", [(i, (i + k) % nb) for i in range(nb)]))
    return got


def per_device(
    outer_gate, inner_gate, signal, filter_in, filter_bias, filter_out, decay, skip_gain
):
    own_rows, width = signal.shape
    nb = lax.axis_size("seq")
    total_rows = own_rows * nb
    s = lax.axis_index("seq")
    count = width // GROUP
    sub = count // nb
    gated_f = lax.reduce_precision(
        inner_gate.astype(jnp.float32) * signal.astype(jnp.float32), exponent_bits=8, mantissa_bits=7)
    gated = gated_f.astype(jnp.bfloat16)
    chunk = sub * GROUP
    pieces = []
    for k in range(nb):
        start = ((s + k) % nb) * chunk
        part = lax.reduce_precision(
            lax.dynamic_slice_in_dim(inner_gate, start, chunk, 1).astype(jnp.float32)
            * lax.dynamic_slice_in_dim(signal, start, chunk, 1).astype(jnp.float32),
            exponent_bits=8, mantissa_bits=7)
        pieces.append(part.astype(jnp.bfloat16).T)
    got = exchange(pieces, nb, s, True)
    positions = jnp.arange(total_rows, dtype=jnp.int32).astype(jnp.float32)
    my_out = lax.dynamic_slice_in_dim(filter_out, s * sub, sub, 1)
    my_decay = lax.dynamic_slice_in_dim(decay, s * sub, sub, 0)
    filters = filter_table(positions, float(total_rows), filter_in, filter_bias, my_out, my_decay)
    lagged = filters.astype(jnp.float32).reshape(nb, own_rows, sub).transpose(0, 2, 1)
    filt = jnp.concatenate([jnp.zeros((1, sub, own_rows), jnp.float32), lagged], axis=0)
    s_arr = jnp.reshape(s, (1,)).astype(jnp.int32)
    conv_parts = toeplitz_conv(s_arr, filt, jnp.stack(got))
    back = exchange(conv_parts, nb, s, True)
    chunks = []
    for c in range(nb):
        src_k = (s - c + nb) % nb
        piece = back[0]
        for k in range(1, nb):
            piece = jnp.where(src_k == k, back[k], piece)
        chunks.append(piece)
    back = jnp.concatenate(chunks, axis=0)
    conv = back.reshape(width, own_rows).T.astype(jnp.float32)
    mixed = outer_gate.astype(jnp.float32) * (conv + skip_gain[None, :] * gated_f)
    return mixed.astype(jnp.bfloat16)


def solution(mesh):
    placed = (
        P(("groups", "seq"), "chan"),
        P(("groups", "seq"), "chan"),
        P(("groups", "seq"), "chan"),
        P(),
        P(),
        P(None, "chan"),
        P("chan"),
        P("chan"),
    )
    return jax.shard_map(
        per_device,
        mesh=mesh,
        in_specs=placed,
        out_specs=P(("groups", "seq"), "chan"),
        check_vma=False,
    )
```
